128 devices in a mesh: group: 2 (over core), member: 64 (over x, z, y).
Axes of the slice: x: 4, y: 4, z: 4, core: 2. Of those that a mesh axis runs over, the one named last changes fastest.
Arguments:
- features: bfloat16 [262144, 256], P(('group', 'member')), may hold values from -6 to 6
- local_home: int32 [8192], P(('group', 'member')), may hold values from 0 to 15
- local_near: int32 [8192], P(('group', 'member')), may hold values from 0 to 15
- local_tiles: bfloat16 [8192, 128, 128], P(('group', 'member')), may hold values from -0.125 to 0.125
- remote_home: int32 [8192], P(('group', 'member')), may hold values from 0 to 15
- remote_far: int32 [8192], P(('group', 'member')), may hold values from 0 to 2047, as said below
- remote_tiles: bfloat16 [8192, 128, 128], P(('group', 'member')), may hold values from -0.125 to 0.125
- weight: bfloat16 [512, 256], replicated, may hold values from -0.25 to 0.25
- cotangent: bfloat16 [262144, 256], P(('group', 'member')), may hold values from -6 to 6
Outputs:
- output: bfloat16 [262144, 256], P(('group', 'member'))
- grad_weight: float32 [512, 256], replicated
- grad_features: float32 [262144, 256], P(('group', 'member'))
The draws below stay inside these ranges and needn't reach their ends.
Inputs may be any that keep to these rules, and one draw needn't show every extreme that they name: `remote_far`: the remote pairs of one owner name partner blocks on 64 different owners other than itself, one block from each owner; one owner, drawn from the seed, holds a partner block of every other owner's remote pairs.
All inputs are finite; a program needn't handle non-finite values.
Results may differ from the reference program's by a relative error of at most 0.0057.
Values may be sent and summed in bfloat16 or wider, within the bound.
No kernel may reach another device: no remote copies, remote signals or barrier semaphores. Data moves between devices by JAX's collectives and lax.ppermute only.
A program may use at most 192 MiB of HBM per device.

```python
import jax
import jax.numpy as jnp
from jax import lax

F = 256
BLOCK = 128
BLK_DEV = 16
LOCAL_DEV = 64
REMOTE_DEV = 64
ITEMS = 262144
DEVICES = 128


def draw_remote_far(key, part):
    target = jax.random.randint(jax.random.fold_in(key, 7), (), 0, DEVICES)
    device_keys = jax.random.split(jax.random.fold_in(key, 11), DEVICES)
    owners = jnp.arange(DEVICES, dtype=jnp.int32)

    def one_device(dev_key, self_index):
        positions = jnp.arange(DEVICES, dtype=jnp.int32)
        scores = jax.random.permutation(dev_key, DEVICES).astype(jnp.int32)
        scores = jnp.where(positions == target, -1, scores)
        scores = jnp.where(positions == self_index, DEVICES + 5, scores)
        chosen = jnp.argsort(scores, stable=True)[:REMOTE_DEV].astype(jnp.int32)
        offset = jax.random.randint(jax.random.fold_in(dev_key, 3), (REMOTE_DEV,), 0, BLK_DEV)
        return (chosen * BLK_DEV + offset).astype(jnp.int32)
    return jax.vmap(one_device)(device_keys, owners).reshape(-1)


def place_ends(entries, rng, low, top_value):
    index_at = [jax.random.randint(jax.random.fold_in(rng, axis), (), 0, length) for axis, length in enumerate(entries.shape)]
    widest = entries.shape.index(max(entries.shape))
    neighbour = index_at[:widest] + [(index_at[widest] + 1) % entries.shape[widest]] + index_at[widest + 1:]
    return entries.at[tuple(index_at)].set(low).at[tuple(neighbour)].set(top_value)


def block_levels(key, extent, cuts, least, high):
    loudness = 1.0
    for axis_at, blocks in cuts:
        heights = jax.random.uniform(jax.random.fold_in(jax.random.fold_in(key, 6), axis_at), (blocks,), jnp.float32, least / len(cuts), high / len(cuts))
        loudness = loudness * jnp.repeat(jnp.exp(heights), extent[axis_at] // blocks).reshape((-1,) + (1,) * (len(extent) - 1 - axis_at))
    return loudness


def bell_draw(rng, shape, width, limit, shards=(), kind=jnp.bfloat16):
    gain = block_levels(rng, shape, shards, -0.22, 0.18) if shards else 1.0
    drawn = jax.random.normal(rng, shape, jnp.float32) * width * gain
    return jnp.minimum(jnp.maximum(drawn, -limit), limit).astype(kind)


def setup_inputs(seed: int = 0) -> dict:
    splits = jax.random.split(jax.random.key(seed), 10)
    features = bell_draw(splits[0], (ITEMS, F), 1.0, 6.0, ((0, 128),))
    local_home = place_ends(jax.random.randint(splits[1], (DEVICES * LOCAL_DEV,), 0, BLK_DEV), jax.random.fold_in(splits[1], 1), 0, BLK_DEV - 1).astype(jnp.int32)
    local_near = place_ends(jax.random.randint(splits[2], (DEVICES * LOCAL_DEV,), 0, BLK_DEV), jax.random.fold_in(splits[2], 1), 0, BLK_DEV - 1).astype(jnp.int32)
    local_tiles = bell_draw(splits[3], (DEVICES * LOCAL_DEV, BLOCK, BLOCK), (BLOCK * 16) ** -0.5, 0.125, ((0, 128),))
    remote_home = place_ends(jax.random.randint(splits[4], (DEVICES * REMOTE_DEV,), 0, BLK_DEV), jax.random.fold_in(splits[4], 1), 0, BLK_DEV - 1).astype(jnp.int32)
    remote_far = draw_remote_far(jax.random.fold_in(splits[9], 71), 0)
    remote_tiles = bell_draw(splits[6], (DEVICES * REMOTE_DEV, BLOCK, BLOCK), (BLOCK * 16) ** -0.5, 0.125, ((0, 128),))
    weight = bell_draw(splits[7], (2 * F, F), (2 * F) ** -0.5, 0.25)
    cotangent = bell_draw(splits[8], (ITEMS, F), 1.0, 6.0, ((0, 128),))
    return {"features": features, "local_home": local_home, "local_near": local_near, "local_tiles": local_tiles, "remote_home": remote_home, "remote_far": remote_far, "remote_tiles": remote_tiles, "weight": weight, "cotangent": cotangent}


def spread(index_list, count):
    return (index_list[:, None] == jnp.arange(count, dtype=jnp.int32)[None, :]).astype(jnp.float32)

def apply_graph(field, local_home, local_near, local_tiles, remote_home, remote_far, remote_tiles):
    field_dev = field.reshape(DEVICES, BLK_DEV, BLOCK, F)
    whole = field.reshape(DEVICES * BLK_DEV, BLOCK, F)
    inputs = (field_dev, local_home.reshape(DEVICES, LOCAL_DEV), local_near.reshape(DEVICES, LOCAL_DEV), local_tiles.reshape(DEVICES, LOCAL_DEV, BLOCK, BLOCK), remote_home.reshape(DEVICES, REMOTE_DEV), remote_far.reshape(DEVICES, REMOTE_DEV), remote_tiles.reshape(DEVICES, REMOTE_DEV, BLOCK, BLOCK))

    def one_owner(far_total, item):
        own, home_l, near_l, tiles_l, home_r, far_r, tiles_r = item
        own_f = own.astype(jnp.float32)
        tl = tiles_l.astype(jnp.float32)
        tr = tiles_r.astype(jnp.float32)
        to_home = jnp.einsum('pab,pbf->paf', tl, own_f[near_l], precision=lax.Precision.HIGHEST)
        to_near = jnp.einsum('pba,pbf->paf', tl, own_f[home_l], precision=lax.Precision.HIGHEST)
        far_vals = whole[far_r].astype(jnp.float32)
        to_home_r = jnp.einsum('pab,pbf->paf', tr, far_vals, precision=lax.Precision.HIGHEST)
        to_far = jnp.einsum('pba,pbf->paf', tr, own_f[home_r], precision=lax.Precision.HIGHEST)
        to_far = to_far.astype(jnp.bfloat16).astype(jnp.float32)
        local_sum = jnp.einsum('pk,paf->kaf', spread(home_l, BLK_DEV), to_home, precision=lax.Precision.HIGHEST)
        local_sum = local_sum + jnp.einsum('pk,paf->kaf', spread(near_l, BLK_DEV), to_near, precision=lax.Precision.HIGHEST)
        local_sum = local_sum + jnp.einsum('pk,paf->kaf', spread(home_r, BLK_DEV), to_home_r, precision=lax.Precision.HIGHEST)
        far_total = far_total.at[far_r].add(to_far)
        return (far_total, local_sum)
    start = jnp.zeros((DEVICES * BLK_DEV, BLOCK, F), jnp.float32)
    far_total, local_sums = lax.scan(one_owner, start, inputs)
    result = local_sums.reshape(DEVICES * BLK_DEV, BLOCK, F) + far_total
    return result.reshape(ITEMS, F)

def reference(features, local_home, local_near, local_tiles, remote_home, remote_far, remote_tiles, weight, cotangent):
    graph_args = (local_home, local_near, local_tiles, remote_home, remote_far, remote_tiles)
    aggregate = apply_graph(features, *graph_args).astype(jnp.bfloat16)
    joined = jnp.concatenate([features, aggregate], axis=1)
    pre_act = jnp.dot(joined, weight, preferred_element_type=jnp.float32)
    sigmoid_z = jax.nn.sigmoid(pre_act)
    output = (pre_act * sigmoid_z).astype(jnp.bfloat16)
    grad_pre = (cotangent.astype(jnp.float32) * sigmoid_z * (1.0 + pre_act * (1.0 - sigmoid_z))).astype(jnp.bfloat16)
    grad_scale = 1.0 / jnp.sqrt(jnp.float32(ITEMS))
    grad_weight = jnp.dot(joined.T, grad_pre, preferred_element_type=jnp.float32) * grad_scale
    grad_joined = jnp.dot(grad_pre, weight.T, preferred_element_type=jnp.float32)
    grad_agg = grad_joined[:, F:].astype(jnp.bfloat16)
    grad_features = grad_joined[:, :F] + apply_graph(grad_agg, *graph_args)
    return (output, grad_weight, grad_features)
```

```python
import math

import jax
import jax.numpy as jnp
from jax import lax
from jax.experimental import pallas as pl
from jax.experimental.pallas import tpu as pltpu
from jax.sharding import PartitionSpec as P

F = 256
BLOCK = 128
BLK_DEV = 16
AXES = ("group", "member")
VMEM_LIMIT = 56 * 1024 * 1024


def _smem():
    return pl.BlockSpec(memory_space=pltpu.SMEM)


def _vmem():
    return pl.BlockSpec(memory_space=pltpu.VMEM)


def _dot_t(a, v):
    return lax.dot_general(a, v, (((0,), (0,)), ((), ())), preferred_element_type=jnp.float32)


def _send_kernel(picked_ref, rhome_ref, tdev_ref, x_ref, rt_ref, send_ref):
    slots = send_ref.shape[0]
    pairs = rt_ref.shape[0]

    def fill(t, c):
        send_ref[t, 0] = x_ref[picked_ref[t]]
        send_ref[t, 1] = jnp.zeros((BLOCK, F), send_ref.dtype)
        return c

    lax.fori_loop(0, slots, fill, 0)

    def term(p, c):
        r = _dot_t(rt_ref[p], x_ref[rhome_ref[p]])
        send_ref[tdev_ref[p], 1] = r.astype(send_ref.dtype)
        return c

    lax.fori_loop(0, pairs, term, 0)


def build_send(picked, rhome, tdev, x, rtiles):
    slots = picked.shape[0]
    return pl.pallas_call(
        _send_kernel,
        out_shape=jax.ShapeDtypeStruct((slots, 2, BLOCK, F), jnp.bfloat16),
        in_specs=[_smem(), _smem(), _smem(), _vmem(), _vmem()],
        out_specs=_vmem(),
        compiler_params=pltpu.CompilerParams(vmem_limit_bytes=VMEM_LIMIT),
    )(picked, rhome, tdev, x, rtiles)


def _gather_kernel(lhome_ref, lnear_ref, rhome_ref, tdev_ref, picked_ref, valid_ref,
                   x_ref, lt_ref, rt_ref, recv_ref, init_ref, out_ref):
    out_ref[...] = init_ref[...]
    n_local = lt_ref.shape[0]
    n_remote = rt_ref.shape[0]
    slots = recv_ref.shape[0]

    def local(p, c):
        h = lhome_ref[p]
        n = lnear_ref[p]
        a = lt_ref[p]
        out_ref[h] += jnp.dot(a, x_ref[n], preferred_element_type=jnp.float32)
        out_ref[n] += _dot_t(a, x_ref[h])
        return c

    lax.fori_loop(0, n_local, local, 0)

    def remote(p, c):
        h = rhome_ref[p]
        out_ref[h] += jnp.dot(rt_ref[p], recv_ref[tdev_ref[p], 0], preferred_element_type=jnp.float32)
        return c

    lax.fori_loop(0, n_remote, remote, 0)

    def back(s, c):
        @pl.when(valid_ref[s] > 0)
        def _():
            k = picked_ref[s]
            out_ref[k] += recv_ref[s, 1].astype(jnp.float32)
        return c

    lax.fori_loop(0, slots, back, 0)


def gather_sum(lhome, lnear, rhome, tdev, picked, valid, x, ltiles, rtiles, recv, init):
    return pl.pallas_call(
        _gather_kernel,
        out_shape=jax.ShapeDtypeStruct(init.shape, jnp.float32),
        in_specs=[_smem()] * 6 + [_vmem()] * 5,
        out_specs=_vmem(),
        compiler_params=pltpu.CompilerParams(vmem_limit_bytes=VMEM_LIMIT),
    )(lhome, lnear, rhome, tdev, picked, valid, x, ltiles, rtiles, recv, init)


def body(
    features,
    local_home,
    local_near,
    local_tiles,
    remote_home,
    remote_far,
    remote_tiles,
    weight,
    cotangent,
):
    device_count = lax.axis_size(AXES)
    row_count = features.shape[0]
    own_blocks = row_count // BLOCK
    lhome = jnp.clip(local_home, 0, own_blocks - 1)
    lnear = jnp.clip(local_near, 0, own_blocks - 1)
    rhome = jnp.clip(remote_home, 0, own_blocks - 1)
    target_dev = jnp.clip(remote_far // BLK_DEV, 0, device_count - 1)
    wanted = remote_far % BLK_DEV
    request = jnp.full((device_count,), -1, jnp.int32).at[target_dev].set(wanted)
    asked = lax.all_to_all(request, AXES, split_axis=0, concat_axis=0, tiled=True)
    picked = jnp.clip(asked, 0, own_blocks - 1)
    valid = (asked >= 0).astype(jnp.int32)

    def apply_graph(blocks_in, init):
        send = build_send(picked, rhome, target_dev, blocks_in, remote_tiles)
        recv = lax.all_to_all(send, AXES, split_axis=0, concat_axis=0, tiled=True)
        total = gather_sum(lhome, lnear, rhome, target_dev, picked, valid,
                           blocks_in, local_tiles, remote_tiles, recv, init)
        return total.reshape(row_count, F)

    zeros = jnp.zeros((own_blocks, BLOCK, F), jnp.float32)
    aggregate = apply_graph(features.reshape(own_blocks, BLOCK, F), zeros).astype(jnp.bfloat16)
    joined = jnp.concatenate([features, aggregate], axis=1)
    pre_act = jnp.dot(joined, weight, preferred_element_type=jnp.float32)
    sigmoid_z = jax.nn.sigmoid(pre_act)
    output = (pre_act * sigmoid_z).astype(jnp.bfloat16)
    grad_pre = (
        cotangent.astype(jnp.float32) * sigmoid_z * (1.0 + pre_act * (1.0 - sigmoid_z))
    ).astype(jnp.bfloat16)
    partial_grad = jnp.einsum("ra,rf->af", joined, grad_pre, preferred_element_type=jnp.float32)
    rows = partial_grad.shape[0]
    chunk = rows // device_count
    pieces = lax.all_to_all(
        partial_grad.reshape(device_count, chunk, F), AXES, split_axis=0, concat_axis=0, tiled=True
    )
    mine = pieces.sum(axis=0)
    spread_out = jnp.broadcast_to(mine[None], (device_count, chunk, F))
    gathered = lax.all_to_all(spread_out, AXES, split_axis=0, concat_axis=0, tiled=True)
    grad_scale = 1.0 / math.sqrt(row_count * device_count)
    grad_weight = gathered.reshape(rows, F) * grad_scale
    grad_joined = jnp.einsum("rf,af->ra", grad_pre, weight, preferred_element_type=jnp.float32)
    grad_agg = grad_joined[:, F:].astype(jnp.bfloat16).reshape(own_blocks, BLOCK, F)
    init_b = grad_joined[:, :F].reshape(own_blocks, BLOCK, F)
    grad_features = apply_graph(grad_agg, init_b)
    return (output, grad_weight, grad_features)


def solution(mesh):
    in_specs = (
        P(AXES, None),
        P(AXES),
        P(AXES),
        P(AXES, None, None),
        P(AXES),
        P(AXES),
        P(AXES, None, None),
        P(),
        P(AXES, None),
    )
    out_specs = (P(AXES, None), P(), P(AXES, None))
    return jax.shard_map(body, mesh=mesh, in_specs=in_specs, out_specs=out_specs, check_vma=False)
```

```python
import math

import jax
import jax.numpy as jnp
from jax import lax
from jax.experimental import pallas as pl
from jax.experimental.pallas import tpu as pltpu
from jax.sharding import PartitionSpec as P

F = 256
BLOCK = 128
BLK_DEV = 16
AXES = ("group", "member")
VMEM_LIMIT = 56 * 1024 * 1024


def _smem():
    return pl.BlockSpec(memory_space=pltpu.SMEM)


def _vmem():
    return pl.BlockSpec(memory_space=pltpu.VMEM)


def _dot_t(a, v):
    return lax.dot_general(a, v, (((0,), (0,)), ((), ())), preferred_element_type=jnp.float32)


def _lists(dest, n_dest):
    order = jnp.argsort(dest, stable=True).astype(jnp.int32)
    counts = jnp.sum(dest[:, None] == jnp.arange(n_dest, dtype=jnp.int32)[None, :], axis=0)
    starts = jnp.concatenate([jnp.zeros((1,), jnp.int32), jnp.cumsum(counts).astype(jnp.int32)])
    return order, starts


def _local_kernel(hs_ref, ho_ref, ns_ref, no_ref, lh_ref, ln_ref, x_ref, lt_ref, init_ref, out_ref):
    blocks = out_ref.shape[0]

    def per_block(k, c):
        acc = init_ref[k]

        def home_term(i, a):
            p = ho_ref[i]
            return a + jnp.dot(lt_ref[p], x_ref[ln_ref[p]], preferred_element_type=jnp.float32)

        acc = lax.fori_loop(hs_ref[k], hs_ref[k + 1], home_term, acc)

        def near_term(i, a):
            p = no_ref[i]
            return a + _dot_t(lt_ref[p], x_ref[lh_ref[p]])

        acc = lax.fori_loop(ns_ref[k], ns_ref[k + 1], near_term, acc)
        out_ref[k] = acc
        return c

    lax.fori_loop(0, blocks, per_block, 0)


def local_sum(hs, ho, ns, no, lh, ln, x, ltiles, init):
    pairs = ltiles.shape[0]
    cost = pl.CostEstimate(
        flops=2 * 2 * pairs * BLOCK * BLOCK * F,
        transcendentals=0,
        bytes_accessed=x.size * 2 + ltiles.size * 2 + init.size * 8,
    )
    return pl.pallas_call(
        _local_kernel,
        out_shape=jax.ShapeDtypeStruct(init.shape, jnp.float32),
        in_specs=[_smem()] * 6 + [_vmem()] * 3,
        out_specs=_vmem(),
        cost_estimate=cost,
        compiler_params=pltpu.CompilerParams(vmem_limit_bytes=VMEM_LIMIT),
    )(hs, ho, ns, no, lh, ln, x, ltiles, init)


SEND_GROUP = 8


def _send_kernel(picked_ref, spair_ref, sused_ref, rhome_ref, x_ref, rt_ref, send_ref):
    base = pl.program_id(0) * SEND_GROUP
    for j in range(SEND_GROUP):
        t = base + j
        send_ref[j, 0] = x_ref[picked_ref[t]]
        p = spair_ref[t]
        r = _dot_t(rt_ref[p], x_ref[rhome_ref[p]])
        r = jnp.where(sused_ref[t] > 0, r, 0.0)
        send_ref[j, 1] = r.astype(send_ref.dtype)


def build_send(picked, spair, sused, rhome, x, rtiles):
    slots = picked.shape[0]
    full3 = lambda i: (0, 0, 0)
    cost = pl.CostEstimate(
        flops=2 * slots * BLOCK * BLOCK * F,
        transcendentals=0,
        bytes_accessed=x.size * 2 + rtiles.size * 2 + slots * 2 * BLOCK * F * 2,
    )
    return pl.pallas_call(
        _send_kernel,
        grid=(slots // SEND_GROUP,),
        out_shape=jax.ShapeDtypeStruct((slots, 2, BLOCK, F), jnp.bfloat16),
        in_specs=[_smem()] * 4 + [
            pl.BlockSpec(x.shape, full3),
            pl.BlockSpec(rtiles.shape, full3),
        ],
        out_specs=pl.BlockSpec((SEND_GROUP, 2, BLOCK, F), lambda i: (i, 0, 0, 0)),
        cost_estimate=cost,
        compiler_params=pltpu.CompilerParams(vmem_limit_bytes=VMEM_LIMIT),
    )(picked, spair, sused, rhome, x, rtiles)


def _post_kernel(rs_ref, ro_ref, td_ref, ss_ref, so_ref, rt_ref, recv_ref, base_ref, out_ref):
    blocks = out_ref.shape[0]

    def per_block(k, c):
        acc = base_ref[k]

        def remote_term(i, a):
            p = ro_ref[i]
            return a + jnp.dot(rt_ref[p], recv_ref[td_ref[p], 0], preferred_element_type=jnp.float32)

        acc = lax.fori_loop(rs_ref[k], rs_ref[k + 1], remote_term, acc)

        def back_term(i, a):
            return a + recv_ref[so_ref[i], 1].astype(jnp.float32)

        acc = lax.fori_loop(ss_ref[k], ss_ref[k + 1], back_term, acc)
        out_ref[k] = acc
        return c

    lax.fori_loop(0, blocks, per_block, 0)


def post_sum(rs, ro, td, ss, so, rtiles, recv, base):
    pairs = rtiles.shape[0]
    cost = pl.CostEstimate(
        flops=2 * pairs * BLOCK * BLOCK * F,
        transcendentals=0,
        bytes_accessed=rtiles.size * 2 + recv.size * 2 + base.size * 8,
    )
    return pl.pallas_call(
        _post_kernel,
        out_shape=jax.ShapeDtypeStruct(base.shape, jnp.float32),
        in_specs=[_smem()] * 5 + [_vmem()] * 3,
        out_specs=_vmem(),
        cost_estimate=cost,
        input_output_aliases={7: 0},
        compiler_params=pltpu.CompilerParams(vmem_limit_bytes=VMEM_LIMIT),
    )(rs, ro, td, ss, so, rtiles, recv, base)


def body(
    features,
    local_home,
    local_near,
    local_tiles,
    remote_home,
    remote_far,
    remote_tiles,
    weight,
    cotangent,
):
    device_count = lax.axis_size(AXES)
    row_count = features.shape[0]
    own_blocks = row_count // BLOCK
    lhome = jnp.clip(local_home, 0, own_blocks - 1)
    lnear = jnp.clip(local_near, 0, own_blocks - 1)
    rhome = jnp.clip(remote_home, 0, own_blocks - 1)
    target_dev = jnp.clip(remote_far // BLK_DEV, 0, device_count - 1)
    wanted = remote_far % BLK_DEV
    request = jnp.full((device_count,), -1, jnp.int32).at[target_dev].set(wanted)
    asked = lax.all_to_all(request, AXES, split_axis=0, concat_axis=0, tiled=True)
    picked = jnp.clip(asked, 0, own_blocks - 1)
    back_dest = jnp.where(asked >= 0, picked, own_blocks)
    slot_pair = jnp.zeros((device_count,), jnp.int32).at[target_dev].set(
        jnp.arange(target_dev.shape[0], dtype=jnp.int32))
    slot_used = jnp.zeros((device_count,), jnp.int32).at[target_dev].set(1)
    h_order, h_starts = _lists(lhome, own_blocks)
    n_order, n_starts = _lists(lnear, own_blocks)
    r_order, r_starts = _lists(rhome, own_blocks)
    s_order, s_starts = _lists(back_dest, own_blocks)

    def apply_graph(blocks_in, init):
        send = build_send(picked, slot_pair, slot_used, rhome, blocks_in, remote_tiles)
        recv = lax.all_to_all(send, AXES, split_axis=0, concat_axis=0, tiled=True)
        part = local_sum(h_starts, h_order, n_starts, n_order, lhome, lnear, blocks_in, local_tiles, init)
        total = post_sum(r_starts, r_order, target_dev, s_starts, s_order, remote_tiles, recv, part)
        return total.reshape(row_count, F)

    zeros = jnp.zeros((own_blocks, BLOCK, F), jnp.float32)
    aggregate = apply_graph(features.reshape(own_blocks, BLOCK, F), zeros).astype(jnp.bfloat16)
    joined = jnp.concatenate([features, aggregate], axis=1)
    pre_act = jnp.dot(joined, weight, preferred_element_type=jnp.float32)
    sigmoid_z = jax.nn.sigmoid(pre_act)
    output = (pre_act * sigmoid_z).astype(jnp.bfloat16)
    grad_pre = (
        cotangent.astype(jnp.float32) * sigmoid_z * (1.0 + pre_act * (1.0 - sigmoid_z))
    ).astype(jnp.bfloat16)
    partial_grad = jnp.einsum("ra,rf->af", joined, grad_pre, preferred_element_type=jnp.float32)
    grad_scale = 1.0 / math.sqrt(row_count * device_count)
    grad_weight = lax.psum(partial_grad, AXES) * grad_scale
    grad_joined = jnp.einsum("rf,af->ra", grad_pre, weight, preferred_element_type=jnp.float32)
    grad_agg = grad_joined[:, F:].astype(jnp.bfloat16).reshape(own_blocks, BLOCK, F)
    init_b = grad_joined[:, :F].reshape(own_blocks, BLOCK, F)
    grad_features = apply_graph(grad_agg, init_b)
    return (output, grad_weight, grad_features)


def solution(mesh):
    in_specs = (
        P(AXES, None),
        P(AXES),
        P(AXES),
        P(AXES, None, None),
        P(AXES),
        P(AXES),
        P(AXES, None, None),
        P(),
        P(AXES, None),
    )
    out_specs = (P(AXES, None), P(), P(AXES, None))
    return jax.shard_map(body, mesh=mesh, in_specs=in_specs, out_specs=out_specs, check_vma=False)
```

```python
import math

import jax
import jax.numpy as jnp
from jax import lax
from jax.experimental import pallas as pl
from jax.experimental.pallas import tpu as pltpu
from jax.sharding import PartitionSpec as P

F = 256
BLOCK = 128
BLK_DEV = 16
AXES = ("group", "member")
VMEM_LIMIT = 56 * 1024 * 1024


def _smem():
    return pl.BlockSpec(memory_space=pltpu.SMEM)


def _vmem():
    return pl.BlockSpec(memory_space=pltpu.VMEM)


def _dot_t(a, v):
    return lax.dot_general(a, v, (((0,), (0,)), ((), ())), preferred_element_type=jnp.float32)


def _lists(dest, n_dest):
    order = jnp.argsort(dest, stable=True).astype(jnp.int32)
    counts = jnp.sum(dest[:, None] == jnp.arange(n_dest, dtype=jnp.int32)[None, :], axis=0)
    starts = jnp.concatenate([jnp.zeros((1,), jnp.int32), jnp.cumsum(counts).astype(jnp.int32)])
    return order, starts


def _local_kernel(hs_ref, ho_ref, ns_ref, no_ref, lh_ref, ln_ref, x_ref, lt_ref, init_ref, out_ref):
    blocks = out_ref.shape[0]

    def per_block(k, c):
        acc = init_ref[k]

        def home_term(i, a):
            p = ho_ref[i]
            return a + jnp.dot(lt_ref[p], x_ref[ln_ref[p]], preferred_element_type=jnp.float32)

        acc = lax.fori_loop(hs_ref[k], hs_ref[k + 1], home_term, acc)

        def near_term(i, a):
            p = no_ref[i]
            return a + _dot_t(lt_ref[p], x_ref[lh_ref[p]])

        acc = lax.fori_loop(ns_ref[k], ns_ref[k + 1], near_term, acc)
        out_ref[k] = acc
        return c

    lax.fori_loop(0, blocks, per_block, 0)


def local_sum(hs, ho, ns, no, lh, ln, x, ltiles, init):
    pairs = ltiles.shape[0]
    cost = pl.CostEstimate(
        flops=2 * 2 * pairs * BLOCK * BLOCK * F,
        transcendentals=0,
        bytes_accessed=x.size * 2 + ltiles.size * 2 + init.size * 8,
    )
    return pl.pallas_call(
        _local_kernel,
        out_shape=jax.ShapeDtypeStruct(init.shape, jnp.float32),
        in_specs=[_smem()] * 6 + [_vmem()] * 3,
        out_specs=_vmem(),
        cost_estimate=cost,
        compiler_params=pltpu.CompilerParams(vmem_limit_bytes=VMEM_LIMIT),
    )(hs, ho, ns, no, lh, ln, x, ltiles, init)


SEND_GROUP = 8


def _send_kernel(picked_ref, spair_ref, sused_ref, rhome_ref, x_ref, rt_ref, *rest):
    send_ref = rest[-1]
    extra_ref = rest[0] if len(rest) == 2 else None
    base = pl.program_id(0) * SEND_GROUP
    for j in range(SEND_GROUP):
        t = base + j
        send_ref[j, pl.ds(0, BLOCK)] = x_ref[picked_ref[t]]
        p = spair_ref[t]
        r = _dot_t(rt_ref[p], x_ref[rhome_ref[p]])
        r = jnp.where(sused_ref[t] > 0, r, 0.0)
        send_ref[j, pl.ds(BLOCK, BLOCK)] = r.astype(send_ref.dtype)
        if extra_ref is not None:
            send_ref[j, pl.ds(2 * BLOCK, extra_ref.shape[1])] = extra_ref[j]


def build_send(picked, spair, sused, rhome, x, rtiles, extra=None):
    slots = picked.shape[0]
    full3 = lambda i: (0, 0, 0)
    extra_rows = 0 if extra is None else extra.shape[1]
    rows = 2 * BLOCK + extra_rows
    cost = pl.CostEstimate(
        flops=2 * slots * BLOCK * BLOCK * F,
        transcendentals=0,
        bytes_accessed=x.size * 2 + rtiles.size * 2 + slots * rows * F * 2,
    )
    in_specs = [_smem()] * 4 + [pl.BlockSpec(x.shape, full3), pl.BlockSpec(rtiles.shape, full3)]
    args = [picked, spair, sused, rhome, x, rtiles]
    if extra is not None:
        in_specs.append(pl.BlockSpec((SEND_GROUP, extra_rows, F), lambda i: (i, 0, 0)))
        args.append(extra)
    return pl.pallas_call(
        _send_kernel,
        grid=(slots // SEND_GROUP,),
        out_shape=jax.ShapeDtypeStruct((slots, rows, F), jnp.bfloat16),
        in_specs=in_specs,
        out_specs=pl.BlockSpec((SEND_GROUP, rows, F), lambda i: (i, 0, 0)),
        cost_estimate=cost,
        compiler_params=pltpu.CompilerParams(vmem_limit_bytes=VMEM_LIMIT),
    )(*args)


def _post_kernel(rs_ref, ro_ref, td_ref, ss_ref, so_ref, rt_ref, recv_ref, base_ref, out_ref):
    blocks = out_ref.shape[0]

    def per_block(k, c):
        acc = base_ref[k]

        def remote_term(i, a):
            p = ro_ref[i]
            return a + jnp.dot(rt_ref[p], recv_ref[td_ref[p], pl.ds(0, BLOCK)], preferred_element_type=jnp.float32)

        acc = lax.fori_loop(rs_ref[k], rs_ref[k + 1], remote_term, acc)

        def back_term(i, a):
            return a + recv_ref[so_ref[i], pl.ds(BLOCK, BLOCK)].astype(jnp.float32)

        acc = lax.fori_loop(ss_ref[k], ss_ref[k + 1], back_term, acc)
        out_ref[k] = acc
        return c

    lax.fori_loop(0, blocks, per_block, 0)


def post_sum(rs, ro, td, ss, so, rtiles, recv, base):
    pairs = rtiles.shape[0]
    cost = pl.CostEstimate(
        flops=2 * pairs * BLOCK * BLOCK * F,
        transcendentals=0,
        bytes_accessed=rtiles.size * 2 + recv.size * 2 + base.size * 8,
    )
    return pl.pallas_call(
        _post_kernel,
        out_shape=jax.ShapeDtypeStruct(base.shape, jnp.float32),
        in_specs=[_smem()] * 5 + [_vmem()] * 3,
        out_specs=_vmem(),
        cost_estimate=cost,
        input_output_aliases={7: 0},
        compiler_params=pltpu.CompilerParams(vmem_limit_bytes=VMEM_LIMIT),
    )(rs, ro, td, ss, so, rtiles, recv, base)


def body(
    features,
    local_home,
    local_near,
    local_tiles,
    remote_home,
    remote_far,
    remote_tiles,
    weight,
    cotangent,
):
    device_count = lax.axis_size(AXES)
    row_count = features.shape[0]
    own_blocks = row_count // BLOCK
    lhome = jnp.clip(local_home, 0, own_blocks - 1)
    lnear = jnp.clip(local_near, 0, own_blocks - 1)
    rhome = jnp.clip(remote_home, 0, own_blocks - 1)
    target_dev = jnp.clip(remote_far // BLK_DEV, 0, device_count - 1)
    wanted = remote_far % BLK_DEV
    request = jnp.full((device_count,), -1, jnp.int32).at[target_dev].set(wanted)
    asked = lax.all_to_all(request, AXES, split_axis=0, concat_axis=0, tiled=True)
    picked = jnp.clip(asked, 0, own_blocks - 1)
    back_dest = jnp.where(asked >= 0, picked, own_blocks)
    slot_pair = jnp.zeros((device_count,), jnp.int32).at[target_dev].set(
        jnp.arange(target_dev.shape[0], dtype=jnp.int32))
    slot_used = jnp.zeros((device_count,), jnp.int32).at[target_dev].set(1)
    h_order, h_starts = _lists(lhome, own_blocks)
    n_order, n_starts = _lists(lnear, own_blocks)
    r_order, r_starts = _lists(rhome, own_blocks)
    s_order, s_starts = _lists(back_dest, own_blocks)

    def apply_graph(blocks_in, init, extra=None):
        send = build_send(picked, slot_pair, slot_used, rhome, blocks_in, remote_tiles, extra)
        recv = lax.all_to_all(send, AXES, split_axis=0, concat_axis=0, tiled=True)
        part = local_sum(h_starts, h_order, n_starts, n_order, lhome, lnear, blocks_in, local_tiles, init)
        total = post_sum(r_starts, r_order, target_dev, s_starts, s_order, remote_tiles, recv, part)
        return total.reshape(row_count, F), recv

    zeros = jnp.zeros((own_blocks, BLOCK, F), jnp.float32)
    aggregate = apply_graph(features.reshape(own_blocks, BLOCK, F), zeros)[0].astype(jnp.bfloat16)
    joined = jnp.concatenate([features, aggregate], axis=1)
    pre_act = jnp.dot(joined, weight, preferred_element_type=jnp.float32)
    sigmoid_z = jax.nn.sigmoid(pre_act)
    output = (pre_act * sigmoid_z).astype(jnp.bfloat16)
    grad_pre = (
        cotangent.astype(jnp.float32) * sigmoid_z * (1.0 + pre_act * (1.0 - sigmoid_z))
    ).astype(jnp.bfloat16)
    partial_grad = jnp.einsum("ra,rf->af", joined, grad_pre, preferred_element_type=jnp.float32)
    rows = partial_grad.shape[0]
    chunk = rows // device_count
    pieces = partial_grad.reshape(device_count, chunk, F)
    pieces_hi = pieces.astype(jnp.bfloat16)
    pieces_lo = (pieces - pieces_hi.astype(jnp.float32)).astype(jnp.bfloat16)
    extra = jnp.concatenate([pieces_hi, pieces_lo], axis=1)
    grad_joined = jnp.einsum("rf,af->ra", grad_pre, weight, preferred_element_type=jnp.float32)
    grad_agg = grad_joined[:, F:].astype(jnp.bfloat16).reshape(own_blocks, BLOCK, F)
    init_b = grad_joined[:, :F].reshape(own_blocks, BLOCK, F)
    grad_features, recv_b = apply_graph(grad_agg, init_b, extra)
    got = recv_b[:, 2 * BLOCK:, :].astype(jnp.float32)
    mine = jnp.sum(got[:, :chunk] + got[:, chunk:], axis=0)
    grad_scale = 1.0 / math.sqrt(row_count * device_count)
    grad_weight = lax.all_gather(mine, AXES, axis=0, tiled=True) * grad_scale
    return (output, grad_weight, grad_features)


def solution(mesh):
    in_specs = (
        P(AXES, None),
        P(AXES),
        P(AXES),
        P(AXES, None, None),
        P(AXES),
        P(AXES),
        P(AXES, None, None),
        P(),
        P(AXES, None),
    )
    out_specs = (P(AXES, None), P(), P(AXES, None))
    return jax.shard_map(body, mesh=mesh, in_specs=in_specs, out_specs=out_specs, check_vma=False)
```

```python
import math

import jax
import jax.numpy as jnp
from jax import lax
from jax.experimental import pallas as pl
from jax.experimental.pallas import tpu as pltpu
from jax.sharding import PartitionSpec as P

F = 256
BLOCK = 128
BLK_DEV = 16
AXES = ("group", "member")
VMEM_LIMIT = 56 * 1024 * 1024


def _smem():
    return pl.BlockSpec(memory_space=pltpu.SMEM)


def _vmem():
    return pl.BlockSpec(memory_space=pltpu.VMEM)


def _dot_t(a, v):
    return lax.dot_general(a, v, (((0,), (0,)), ((), ())), preferred_element_type=jnp.float32)


def _lists(dest, n_dest):
    order = jnp.argsort(dest, stable=True).astype(jnp.int32)
    counts = jnp.sum(dest[:, None] == jnp.arange(n_dest, dtype=jnp.int32)[None, :], axis=0)
    starts = jnp.concatenate([jnp.zeros((1,), jnp.int32), jnp.cumsum(counts).astype(jnp.int32)])
    return order, starts


def _local_kernel(hs_ref, ho_ref, ns_ref, no_ref, lh_ref, ln_ref, x_ref, lt_ref, init_ref, out_ref):
    blocks = out_ref.shape[0]

    def per_block(k, c):
        acc = init_ref[k]

        def home_term(i, a):
            p = ho_ref[i]
            return a + jnp.dot(lt_ref[p], x_ref[ln_ref[p]], preferred_element_type=jnp.float32)

        acc = lax.fori_loop(hs_ref[k], hs_ref[k + 1], home_term, acc)

        def near_term(i, a):
            p = no_ref[i]
            return a + _dot_t(lt_ref[p], x_ref[lh_ref[p]])

        acc = lax.fori_loop(ns_ref[k], ns_ref[k + 1], near_term, acc)
        out_ref[k] = acc
        return c

    lax.fori_loop(0, blocks, per_block, 0)


def local_sum(hs, ho, ns, no, lh, ln, x, ltiles, init):
    pairs = ltiles.shape[0]
    cost = pl.CostEstimate(
        flops=2 * 2 * pairs * BLOCK * BLOCK * F,
        transcendentals=0,
        bytes_accessed=x.size * 2 + ltiles.size * 2 + init.size * 8,
    )
    return pl.pallas_call(
        _local_kernel,
        out_shape=jax.ShapeDtypeStruct(init.shape, jnp.float32),
        in_specs=[_smem()] * 6 + [_vmem()] * 3,
        out_specs=_vmem(),
        cost_estimate=cost,
        compiler_params=pltpu.CompilerParams(vmem_limit_bytes=VMEM_LIMIT),
    )(hs, ho, ns, no, lh, ln, x, ltiles, init)


SEND_GROUP = 8


def _send_kernel(picked_ref, spair_ref, sused_ref, rhome_ref, x_ref, rt_ref, *rest):
    send_ref = rest[-1]
    extra_ref = rest[0] if len(rest) == 2 else None
    base = pl.program_id(0) * SEND_GROUP
    for j in range(SEND_GROUP):
        t = base + j
        send_ref[j, pl.ds(0, BLOCK)] = x_ref[picked_ref[t]]
        p = spair_ref[t]
        r = _dot_t(rt_ref[p], x_ref[rhome_ref[p]])
        r = jnp.where(sused_ref[t] > 0, r, 0.0)
        send_ref[j, pl.ds(BLOCK, BLOCK)] = r.astype(send_ref.dtype)
        if extra_ref is not None:
            send_ref[j, pl.ds(2 * BLOCK, extra_ref.shape[1])] = extra_ref[j]


def build_send(picked, spair, sused, rhome, x, rtiles, extra=None):
    slots = picked.shape[0]
    full3 = lambda i: (0, 0, 0)
    extra_rows = 0 if extra is None else extra.shape[1]
    rows = 2 * BLOCK + extra_rows
    cost = pl.CostEstimate(
        flops=2 * slots * BLOCK * BLOCK * F,
        transcendentals=0,
        bytes_accessed=x.size * 2 + rtiles.size * 2 + slots * rows * F * 2,
    )
    in_specs = [_smem()] * 4 + [pl.BlockSpec(x.shape, full3), pl.BlockSpec(rtiles.shape, full3)]
    args = [picked, spair, sused, rhome, x, rtiles]
    if extra is not None:
        in_specs.append(pl.BlockSpec((SEND_GROUP, extra_rows, F), lambda i: (i, 0, 0)))
        args.append(extra)
    return pl.pallas_call(
        _send_kernel,
        grid=(slots // SEND_GROUP,),
        out_shape=jax.ShapeDtypeStruct((slots, rows, F), jnp.bfloat16),
        in_specs=in_specs,
        out_specs=pl.BlockSpec((SEND_GROUP, rows, F), lambda i: (i, 0, 0)),
        cost_estimate=cost,
        compiler_params=pltpu.CompilerParams(vmem_limit_bytes=VMEM_LIMIT),
    )(*args)


def _post_kernel(rs_ref, ro_ref, td_ref, ss_ref, so_ref, rt_ref, recv_ref, base_ref, out_ref):
    blocks = out_ref.shape[0]

    def per_block(k, c):
        acc = base_ref[k]

        def remote_term(i, a):
            p = ro_ref[i]
            return a + jnp.dot(rt_ref[p], recv_ref[td_ref[p], pl.ds(0, BLOCK)], preferred_element_type=jnp.float32)

        acc = lax.fori_loop(rs_ref[k], rs_ref[k + 1], remote_term, acc)

        def back_term(i, a):
            return a + recv_ref[so_ref[i], pl.ds(BLOCK, BLOCK)].astype(jnp.float32)

        acc = lax.fori_loop(ss_ref[k], ss_ref[k + 1], back_term, acc)
        out_ref[k] = acc
        return c

    lax.fori_loop(0, blocks, per_block, 0)


def post_sum(rs, ro, td, ss, so, rtiles, recv, base):
    pairs = rtiles.shape[0]
    cost = pl.CostEstimate(
        flops=2 * pairs * BLOCK * BLOCK * F,
        transcendentals=0,
        bytes_accessed=rtiles.size * 2 + recv.size * 2 + base.size * 8,
    )
    return pl.pallas_call(
        _post_kernel,
        out_shape=jax.ShapeDtypeStruct(base.shape, jnp.float32),
        in_specs=[_smem()] * 5 + [_vmem()] * 3,
        out_specs=_vmem(),
        cost_estimate=cost,
        input_output_aliases={7: 0},
        compiler_params=pltpu.CompilerParams(vmem_limit_bytes=VMEM_LIMIT),
    )(rs, ro, td, ss, so, rtiles, recv, base)


def body(
    features,
    local_home,
    local_near,
    local_tiles,
    remote_home,
    remote_far,
    remote_tiles,
    weight,
    cotangent,
):
    device_count = lax.axis_size(AXES)
    row_count = features.shape[0]
    own_blocks = row_count // BLOCK
    lhome = jnp.clip(local_home, 0, own_blocks - 1)
    lnear = jnp.clip(local_near, 0, own_blocks - 1)
    rhome = jnp.clip(remote_home, 0, own_blocks - 1)
    target_dev = jnp.clip(remote_far // BLK_DEV, 0, device_count - 1)
    wanted = remote_far % BLK_DEV
    request = jnp.full((device_count,), -1, jnp.int32).at[target_dev].set(wanted)
    asked = lax.all_to_all(request, AXES, split_axis=0, concat_axis=0, tiled=True)
    picked = jnp.clip(asked, 0, own_blocks - 1)
    back_dest = jnp.where(asked >= 0, picked, own_blocks)
    slot_pair = jnp.zeros((device_count,), jnp.int32).at[target_dev].set(
        jnp.arange(target_dev.shape[0], dtype=jnp.int32))
    slot_used = jnp.zeros((device_count,), jnp.int32).at[target_dev].set(1)
    h_order, h_starts = _lists(lhome, own_blocks)
    n_order, n_starts = _lists(lnear, own_blocks)
    r_order, r_starts = _lists(rhome, own_blocks)
    s_order, s_starts = _lists(back_dest, own_blocks)

    def apply_graph(blocks_in, init, extra=None):
        send = build_send(picked, slot_pair, slot_used, rhome, blocks_in, remote_tiles, extra)
        recv = lax.all_to_all(send, AXES, split_axis=0, concat_axis=0, tiled=True)
        part = local_sum(h_starts, h_order, n_starts, n_order, lhome, lnear, blocks_in, local_tiles, init)
        total = post_sum(r_starts, r_order, target_dev, s_starts, s_order, remote_tiles, recv, part)
        return total.reshape(row_count, F), recv

    zeros = jnp.zeros((own_blocks, BLOCK, F), jnp.float32)
    aggregate = apply_graph(features.reshape(own_blocks, BLOCK, F), zeros)[0].astype(jnp.bfloat16)
    joined = jnp.concatenate([features, aggregate], axis=1)
    pre_act = jnp.dot(joined, weight, preferred_element_type=jnp.float32)
    sigmoid_z = jax.nn.sigmoid(pre_act)
    output = (pre_act * sigmoid_z).astype(jnp.bfloat16)
    grad_pre = (
        cotangent.astype(jnp.float32) * sigmoid_z * (1.0 + pre_act * (1.0 - sigmoid_z))
    ).astype(jnp.bfloat16)
    partial_grad = jnp.einsum("ra,rf->af", joined, grad_pre, preferred_element_type=jnp.float32)
    rows = partial_grad.shape[0]
    chunk = rows // device_count
    pieces = partial_grad.reshape(device_count, chunk, F)
    hi_f32 = lax.reduce_precision(pieces, exponent_bits=8, mantissa_bits=7)
    pieces_hi = hi_f32.astype(jnp.bfloat16)
    pieces_lo = (pieces - hi_f32).astype(jnp.bfloat16)
    extra = jnp.concatenate([pieces_hi, pieces_lo], axis=1)
    grad_joined = jnp.einsum("rf,af->ra", grad_pre, weight, preferred_element_type=jnp.float32)
    grad_agg = grad_joined[:, F:].astype(jnp.bfloat16).reshape(own_blocks, BLOCK, F)
    init_b = grad_joined[:, :F].reshape(own_blocks, BLOCK, F)
    grad_features, recv_b = apply_graph(grad_agg, init_b, extra)
    got = recv_b[:, 2 * BLOCK:, :].astype(jnp.float32)
    mine = jnp.sum(got[:, :chunk] + got[:, chunk:], axis=0)
    mine, grad_features = lax.optimization_barrier((mine, grad_features))
    grad_scale = 1.0 / math.sqrt(row_count * device_count)
    spread_out = jnp.broadcast_to(mine[None], (device_count, chunk, F))
    gathered = lax.all_to_all(spread_out, AXES, split_axis=0, concat_axis=0, tiled=True)
    grad_weight = gathered.reshape(rows, F) * grad_scale
    return (output, grad_weight, grad_features)


def solution(mesh):
    in_specs = (
        P(AXES, None),
        P(AXES),
        P(AXES),
        P(AXES, None, None),
        P(AXES),
        P(AXES),
        P(AXES, None, None),
        P(),
        P(AXES, None),
    )
    out_specs = (P(AXES, None), P(), P(AXES, None))
    return jax.shard_map(body, mesh=mesh, in_specs=in_specs, out_specs=out_specs, check_vma=False)
```

```python
import math

import jax
import jax.numpy as jnp
from jax import lax
from jax.experimental import pallas as pl
from jax.experimental.pallas import tpu as pltpu
from jax.sharding import PartitionSpec as P

F = 256
BLOCK = 128
BLK_DEV = 16
AXES = ("group", "member")
SLOT_AXES = ("member", "group")
VMEM_LIMIT = 56 * 1024 * 1024


def _smem():
    return pl.BlockSpec(memory_space=pltpu.SMEM)


def _vmem():
    return pl.BlockSpec(memory_space=pltpu.VMEM)


def _dot_t(a, v):
    return lax.dot_general(a, v, (((0,), (0,)), ((), ())), preferred_element_type=jnp.float32)


def _lists(dest, n_dest):
    order = jnp.argsort(dest, stable=True).astype(jnp.int32)
    counts = jnp.sum(dest[:, None] == jnp.arange(n_dest, dtype=jnp.int32)[None, :], axis=0)
    starts = jnp.concatenate([jnp.zeros((1,), jnp.int32), jnp.cumsum(counts).astype(jnp.int32)])
    return order, starts


def _pair_loop(lo, hi, term, acc):
    count = hi - lo
    iters = (count + 1) // 2

    def step(i, a):
        i0 = lo + 2 * i
        i1 = i0 + 1
        return a + term(i0, jnp.minimum(i1, hi - 1), i1 < hi)

    return lax.fori_loop(0, iters, step, acc)


def _local_kernel(hs_ref, ho_ref, ns_ref, no_ref, lh_ref, ln_ref, x_ref, lt_ref, init_ref, out_ref):
    blocks = out_ref.shape[0]

    def per_block(k, c):
        acc = init_ref[k]

        def home_term(i0, i1, ok):
            p0 = ho_ref[i0]
            p1 = ho_ref[i1]
            lhs = jnp.concatenate([lt_ref[p0], lt_ref[p1]], axis=1)
            v1 = jnp.where(ok, x_ref[ln_ref[p1]], jnp.zeros((BLOCK, F), x_ref.dtype))
            rhs = jnp.concatenate([x_ref[ln_ref[p0]], v1], axis=0)
            return jnp.dot(lhs, rhs, preferred_element_type=jnp.float32)

        acc = _pair_loop(hs_ref[k], hs_ref[k + 1], home_term, acc)

        def near_term(i0, i1, ok):
            p0 = no_ref[i0]
            p1 = no_ref[i1]
            lhs = jnp.concatenate([lt_ref[p0], lt_ref[p1]], axis=0)
            v1 = jnp.where(ok, x_ref[lh_ref[p1]], jnp.zeros((BLOCK, F), x_ref.dtype))
            rhs = jnp.concatenate([x_ref[lh_ref[p0]], v1], axis=0)
            return _dot_t(lhs, rhs)

        acc = _pair_loop(ns_ref[k], ns_ref[k + 1], near_term, acc)
        out_ref[k] = acc
        return c

    lax.fori_loop(0, blocks, per_block, 0)


def local_sum(hs, ho, ns, no, lh, ln, x, ltiles, init):
    pairs = ltiles.shape[0]
    cost = pl.CostEstimate(
        flops=2 * 2 * pairs * BLOCK * BLOCK * F,
        transcendentals=0,
        bytes_accessed=x.size * 2 + ltiles.size * 2 + init.size * 8,
    )
    return pl.pallas_call(
        _local_kernel,
        out_shape=jax.ShapeDtypeStruct(init.shape, jnp.float32),
        in_specs=[_smem()] * 6 + [_vmem()] * 3,
        out_specs=_vmem(),
        cost_estimate=cost,
        compiler_params=pltpu.CompilerParams(vmem_limit_bytes=VMEM_LIMIT),
    )(hs, ho, ns, no, lh, ln, x, ltiles, init)


SEND_GROUP = 8


def _send_kernel(picked_ref, spair_ref, sused_ref, rhome_ref, x_ref, rt_ref, *rest):
    send_ref = rest[-1]
    extra_ref = rest[0] if len(rest) == 2 else None
    base = pl.program_id(0) * SEND_GROUP
    for j in range(SEND_GROUP):
        t = base + j
        send_ref[j, pl.ds(0, BLOCK)] = x_ref[picked_ref[t]]
        p = spair_ref[t]
        r = _dot_t(rt_ref[p], x_ref[rhome_ref[p]])
        r = jnp.where(sused_ref[t] > 0, r, 0.0)
        send_ref[j, pl.ds(BLOCK, BLOCK)] = r.astype(send_ref.dtype)
        if extra_ref is not None:
            send_ref[j, pl.ds(2 * BLOCK, extra_ref.shape[1])] = extra_ref[j]


def build_send(picked, spair, sused, rhome, x, rtiles, extra=None):
    slots = picked.shape[0]
    full3 = lambda i: (0, 0, 0)
    extra_rows = 0 if extra is None else extra.shape[1]
    rows = 2 * BLOCK + extra_rows
    cost = pl.CostEstimate(
        flops=2 * slots * BLOCK * BLOCK * F,
        transcendentals=0,
        bytes_accessed=x.size * 2 + rtiles.size * 2 + slots * rows * F * 2,
    )
    in_specs = [_smem()] * 4 + [pl.BlockSpec(x.shape, full3), pl.BlockSpec(rtiles.shape, full3)]
    args = [picked, spair, sused, rhome, x, rtiles]
    if extra is not None:
        in_specs.append(pl.BlockSpec((SEND_GROUP, extra_rows, F), lambda i: (i, 0, 0)))
        args.append(extra)
    return pl.pallas_call(
        _send_kernel,
        grid=(slots // SEND_GROUP,),
        out_shape=jax.ShapeDtypeStruct((slots, rows, F), jnp.bfloat16),
        in_specs=in_specs,
        out_specs=pl.BlockSpec((SEND_GROUP, rows, F), lambda i: (i, 0, 0)),
        cost_estimate=cost,
        compiler_params=pltpu.CompilerParams(vmem_limit_bytes=VMEM_LIMIT),
    )(*args)


def _post_kernel(rs_ref, ro_ref, td_ref, ss_ref, so_ref, rt_ref, recv_ref, base_ref, out_ref):
    blocks = out_ref.shape[0]

    def per_block(k, c):
        acc = base_ref[k]

        def remote_term(i0, i1, ok):
            p0 = ro_ref[i0]
            p1 = ro_ref[i1]
            lhs = jnp.concatenate([rt_ref[p0], rt_ref[p1]], axis=1)
            v1 = jnp.where(ok, recv_ref[td_ref[p1], pl.ds(0, BLOCK)], jnp.zeros((BLOCK, F), recv_ref.dtype))
            rhs = jnp.concatenate([recv_ref[td_ref[p0], pl.ds(0, BLOCK)], v1], axis=0)
            return jnp.dot(lhs, rhs, preferred_element_type=jnp.float32)

        acc = _pair_loop(rs_ref[k], rs_ref[k + 1], remote_term, acc)

        def back_term(i, a):
            return a + recv_ref[so_ref[i], pl.ds(BLOCK, BLOCK)].astype(jnp.float32)

        acc = lax.fori_loop(ss_ref[k], ss_ref[k + 1], back_term, acc)
        out_ref[k] = acc
        return c

    lax.fori_loop(0, blocks, per_block, 0)


def post_sum(rs, ro, td, ss, so, rtiles, recv, base):
    pairs = rtiles.shape[0]
    cost = pl.CostEstimate(
        flops=2 * pairs * BLOCK * BLOCK * F,
        transcendentals=0,
        bytes_accessed=rtiles.size * 2 + recv.size * 2 + base.size * 8,
    )
    return pl.pallas_call(
        _post_kernel,
        out_shape=jax.ShapeDtypeStruct(base.shape, jnp.float32),
        in_specs=[_smem()] * 5 + [_vmem()] * 3,
        out_specs=_vmem(),
        cost_estimate=cost,
        input_output_aliases={7: 0},
        compiler_params=pltpu.CompilerParams(vmem_limit_bytes=VMEM_LIMIT),
    )(rs, ro, td, ss, so, rtiles, recv, base)


def body(
    features,
    local_home,
    local_near,
    local_tiles,
    remote_home,
    remote_far,
    remote_tiles,
    weight,
    cotangent,
):
    device_count = lax.axis_size(AXES)
    row_count = features.shape[0]
    own_blocks = row_count // BLOCK
    lhome = jnp.clip(local_home, 0, own_blocks - 1)
    lnear = jnp.clip(local_near, 0, own_blocks - 1)
    rhome = jnp.clip(remote_home, 0, own_blocks - 1)
    target_dev = jnp.clip(remote_far // BLK_DEV, 0, device_count - 1)
    wanted = remote_far % BLK_DEV
    request = jnp.full((device_count,), -1, jnp.int32).at[target_dev].set(wanted)
    asked = lax.all_to_all(request, AXES, split_axis=0, concat_axis=0, tiled=True)
    picked_dev = jnp.clip(asked, 0, own_blocks - 1)
    back_dev = jnp.where(asked >= 0, picked_dev, own_blocks)
    groups = lax.axis_size("group")
    members = lax.axis_size("member")
    slot_ids = jnp.arange(device_count, dtype=jnp.int32)
    dev_of_slot = (slot_ids % groups) * members + slot_ids // groups
    target_slot = (target_dev % members) * groups + target_dev // members
    picked = picked_dev[dev_of_slot]
    back_dest = back_dev[dev_of_slot]
    slot_pair = jnp.zeros((device_count,), jnp.int32).at[target_slot].set(
        jnp.arange(target_dev.shape[0], dtype=jnp.int32))
    slot_used = jnp.zeros((device_count,), jnp.int32).at[target_slot].set(1)
    h_order, h_starts = _lists(lhome, own_blocks)
    n_order, n_starts = _lists(lnear, own_blocks)
    r_order, r_starts = _lists(rhome, own_blocks)
    s_order, s_starts = _lists(back_dest, own_blocks)

    def apply_graph(blocks_in, init, extra=None):
        send = build_send(picked, slot_pair, slot_used, rhome, blocks_in, remote_tiles, extra)
        recv = lax.all_to_all(send, SLOT_AXES, split_axis=0, concat_axis=0, tiled=True)
        part = local_sum(h_starts, h_order, n_starts, n_order, lhome, lnear, blocks_in, local_tiles, init)
        total = post_sum(r_starts, r_order, target_slot, s_starts, s_order, remote_tiles, recv, part)
        return total.reshape(row_count, F), recv

    zeros = jnp.zeros((own_blocks, BLOCK, F), jnp.float32)
    aggregate = apply_graph(features.reshape(own_blocks, BLOCK, F), zeros)[0].astype(jnp.bfloat16)
    joined = jnp.concatenate([features, aggregate], axis=1)
    pre_act = jnp.dot(joined, weight, preferred_element_type=jnp.float32)
    sigmoid_z = jax.nn.sigmoid(pre_act)
    output = (pre_act * sigmoid_z).astype(jnp.bfloat16)
    grad_pre = (
        cotangent.astype(jnp.float32) * sigmoid_z * (1.0 + pre_act * (1.0 - sigmoid_z))
    ).astype(jnp.bfloat16)
    partial_grad = jnp.einsum("ra,rf->af", joined, grad_pre, preferred_element_type=jnp.float32)
    rows = partial_grad.shape[0]
    chunk = rows // device_count
    pieces = partial_grad.reshape(device_count, chunk, F)[dev_of_slot]
    hi_f32 = lax.reduce_precision(pieces, exponent_bits=8, mantissa_bits=7)
    pieces_hi = hi_f32.astype(jnp.bfloat16)
    pieces_lo = (pieces - hi_f32).astype(jnp.bfloat16)
    extra = jnp.concatenate([pieces_hi, pieces_lo], axis=1)
    grad_joined = jnp.einsum("rf,af->ra", grad_pre, weight, preferred_element_type=jnp.float32)
    grad_agg = grad_joined[:, F:].astype(jnp.bfloat16).reshape(own_blocks, BLOCK, F)
    init_b = grad_joined[:, :F].reshape(own_blocks, BLOCK, F)
    grad_features, recv_b = apply_graph(grad_agg, init_b, extra)
    got = recv_b[:, 2 * BLOCK:, :].astype(jnp.float32)
    mine = jnp.sum(got[:, :chunk] + got[:, chunk:], axis=0)
    mine, grad_features = lax.optimization_barrier((mine, grad_features))
    grad_scale = 1.0 / math.sqrt(row_count * device_count)
    spread_out = jnp.broadcast_to(mine[None], (device_count, chunk, F))
    gathered = lax.all_to_all(spread_out, AXES, split_axis=0, concat_axis=0, tiled=True)
    grad_weight = gathered.reshape(rows, F) * grad_scale
    return (output, grad_weight, grad_features)


def solution(mesh):
    in_specs = (
        P(AXES, None),
        P(AXES),
        P(AXES),
        P(AXES, None, None),
        P(AXES),
        P(AXES),
        P(AXES, None, None),
        P(),
        P(AXES, None),
    )
    out_specs = (P(AXES, None), P(), P(AXES, None))
    return jax.shard_map(body, mesh=mesh, in_specs=in_specs, out_specs=out_specs, check_vma=False)
```

```python
import math

import jax
import jax.numpy as jnp
from jax import lax
from jax.experimental import pallas as pl
from jax.experimental.pallas import tpu as pltpu
from jax.sharding import PartitionSpec as P

F = 256
BLOCK = 128
BLK_DEV = 16
AXES = ("group", "member")
SLOT_AXES = ("member", "group")
VMEM_LIMIT = 56 * 1024 * 1024


def _smem():
    return pl.BlockSpec(memory_space=pltpu.SMEM)


def _vmem():
    return pl.BlockSpec(memory_space=pltpu.VMEM)


def _dot_t(a, v):
    return lax.dot_general(a, v, (((0,), (0,)), ((), ())), preferred_element_type=jnp.float32)


def _lists(dest, n_dest):
    order = jnp.argsort(dest, stable=True).astype(jnp.int32)
    counts = jnp.sum(dest[:, None] == jnp.arange(n_dest, dtype=jnp.int32)[None, :], axis=0)
    starts = jnp.concatenate([jnp.zeros((1,), jnp.int32), jnp.cumsum(counts).astype(jnp.int32)])
    return order, starts


def _pair_loop(lo, hi, term, acc):
    count = hi - lo
    iters = (count + 1) // 2

    def step(i, a):
        i0 = lo + 2 * i
        i1 = i0 + 1
        return a + term(i0, jnp.minimum(i1, hi - 1), i1 < hi)

    return lax.fori_loop(0, iters, step, acc)


def _local_kernel(hs_ref, ho_ref, ns_ref, no_ref, lh_ref, ln_ref, x_ref, lt_ref, ltt_ref, init_ref, out_ref):
    blocks = out_ref.shape[0]

    def per_block(k, c):
        acc = init_ref[k]

        def home_term(i0, i1, ok):
            p0 = ho_ref[i0]
            p1 = ho_ref[i1]
            lhs = jnp.concatenate([lt_ref[p0], lt_ref[p1]], axis=1)
            v1 = jnp.where(ok, x_ref[ln_ref[p1]], jnp.zeros((BLOCK, F), x_ref.dtype))
            rhs = jnp.concatenate([x_ref[ln_ref[p0]], v1], axis=0)
            return jnp.dot(lhs, rhs, preferred_element_type=jnp.float32)

        acc = _pair_loop(hs_ref[k], hs_ref[k + 1], home_term, acc)

        def near_term(i0, i1, ok):
            p0 = no_ref[i0]
            p1 = no_ref[i1]
            lhs = jnp.concatenate([ltt_ref[p0], ltt_ref[p1]], axis=1)
            v1 = jnp.where(ok, x_ref[lh_ref[p1]], jnp.zeros((BLOCK, F), x_ref.dtype))
            rhs = jnp.concatenate([x_ref[lh_ref[p0]], v1], axis=0)
            return jnp.dot(lhs, rhs, preferred_element_type=jnp.float32)

        acc = _pair_loop(ns_ref[k], ns_ref[k + 1], near_term, acc)
        out_ref[k] = acc
        return c

    lax.fori_loop(0, blocks, per_block, 0)


def local_sum(hs, ho, ns, no, lh, ln, x, ltiles, lttiles, init):
    pairs = ltiles.shape[0]
    cost = pl.CostEstimate(
        flops=2 * 2 * pairs * BLOCK * BLOCK * F,
        transcendentals=0,
        bytes_accessed=x.size * 2 + ltiles.size * 2 + init.size * 8,
    )
    return pl.pallas_call(
        _local_kernel,
        out_shape=jax.ShapeDtypeStruct(init.shape, jnp.float32),
        in_specs=[_smem()] * 6 + [_vmem()] * 4,
        out_specs=_vmem(),
        cost_estimate=cost,
        compiler_params=pltpu.CompilerParams(vmem_limit_bytes=VMEM_LIMIT),
    )(hs, ho, ns, no, lh, ln, x, ltiles, lttiles, init)


SEND_GROUP = 16


def _send_kernel(picked_ref, spair_ref, sused_ref, rhome_ref, x_ref, rt_ref, *rest):
    send_ref = rest[-1]
    extra_ref = rest[0] if len(rest) == 2 else None
    group = send_ref.shape[0]
    base = pl.program_id(0) * group
    for j in range(group):
        t = base + j
        send_ref[j, pl.ds(0, BLOCK)] = x_ref[picked_ref[t]]
        p = spair_ref[t]
        r = jnp.dot(rt_ref[p], x_ref[rhome_ref[p]], preferred_element_type=jnp.float32)
        r = jnp.where(sused_ref[t] > 0, r, 0.0)
        send_ref[j, pl.ds(BLOCK, BLOCK)] = r.astype(send_ref.dtype)
        if extra_ref is not None:
            send_ref[j, pl.ds(2 * BLOCK, extra_ref.shape[1])] = extra_ref[j]


def build_send(picked, spair, sused, rhome, x, rtiles, extra=None):
    slots = picked.shape[0]
    group = math.gcd(SEND_GROUP, slots)
    full3 = lambda i: (0, 0, 0)
    extra_rows = 0 if extra is None else extra.shape[1]
    rows = 2 * BLOCK + extra_rows
    cost = pl.CostEstimate(
        flops=2 * slots * BLOCK * BLOCK * F,
        transcendentals=0,
        bytes_accessed=x.size * 2 + rtiles.size * 2 + slots * rows * F * 2,
    )
    in_specs = [_smem()] * 4 + [pl.BlockSpec(x.shape, full3), pl.BlockSpec(rtiles.shape, full3)]
    args = [picked, spair, sused, rhome, x, rtiles]
    if extra is not None:
        in_specs.append(pl.BlockSpec((group, extra_rows, F), lambda i: (i, 0, 0)))
        args.append(extra)
    return pl.pallas_call(
        _send_kernel,
        grid=(slots // group,),
        out_shape=jax.ShapeDtypeStruct((slots, rows, F), jnp.bfloat16),
        in_specs=in_specs,
        out_specs=pl.BlockSpec((group, rows, F), lambda i: (i, 0, 0)),
        cost_estimate=cost,
        compiler_params=pltpu.CompilerParams(vmem_limit_bytes=VMEM_LIMIT),
    )(*args)


def _post_kernel(rs_ref, ro_ref, td_ref, ss_ref, so_ref, rt_ref, recv_ref, base_ref, out_ref):
    blocks = out_ref.shape[0]

    def per_block(k, c):
        acc = base_ref[k]

        def remote_term(i0, i1, ok):
            p0 = ro_ref[i0]
            p1 = ro_ref[i1]
            lhs = jnp.concatenate([rt_ref[p0], rt_ref[p1]], axis=1)
            v1 = jnp.where(ok, recv_ref[td_ref[p1], pl.ds(0, BLOCK)], jnp.zeros((BLOCK, F), recv_ref.dtype))
            rhs = jnp.concatenate([recv_ref[td_ref[p0], pl.ds(0, BLOCK)], v1], axis=0)
            return jnp.dot(lhs, rhs, preferred_element_type=jnp.float32)

        acc = _pair_loop(rs_ref[k], rs_ref[k + 1], remote_term, acc)

        def back_term(i, a):
            return a + recv_ref[so_ref[i], pl.ds(BLOCK, BLOCK)].astype(jnp.float32)

        acc = lax.fori_loop(ss_ref[k], ss_ref[k + 1], back_term, acc)
        out_ref[k] = acc
        return c

    lax.fori_loop(0, blocks, per_block, 0)


def post_sum(rs, ro, td, ss, so, rtiles, recv, base):
    pairs = rtiles.shape[0]
    cost = pl.CostEstimate(
        flops=2 * pairs * BLOCK * BLOCK * F,
        transcendentals=0,
        bytes_accessed=rtiles.size * 2 + recv.size * 2 + base.size * 8,
    )
    return pl.pallas_call(
        _post_kernel,
        out_shape=jax.ShapeDtypeStruct(base.shape, jnp.float32),
        in_specs=[_smem()] * 5 + [_vmem()] * 3,
        out_specs=_vmem(),
        cost_estimate=cost,
        input_output_aliases={7: 0},
        compiler_params=pltpu.CompilerParams(vmem_limit_bytes=VMEM_LIMIT),
    )(rs, ro, td, ss, so, rtiles, recv, base)


def body(
    features,
    local_home,
    local_near,
    local_tiles,
    remote_home,
    remote_far,
    remote_tiles,
    weight,
    cotangent,
):
    device_count = lax.axis_size(AXES)
    row_count = features.shape[0]
    own_blocks = row_count // BLOCK
    lhome = jnp.clip(local_home, 0, own_blocks - 1)
    lnear = jnp.clip(local_near, 0, own_blocks - 1)
    rhome = jnp.clip(remote_home, 0, own_blocks - 1)
    target_dev = jnp.clip(remote_far // BLK_DEV, 0, device_count - 1)
    wanted = remote_far % BLK_DEV
    request = jnp.full((device_count,), -1, jnp.int32).at[target_dev].set(wanted)
    asked = lax.all_to_all(request, AXES, split_axis=0, concat_axis=0, tiled=True)
    picked_dev = jnp.clip(asked, 0, own_blocks - 1)
    back_dev = jnp.where(asked >= 0, picked_dev, own_blocks)
    groups = lax.axis_size("group")
    members = lax.axis_size("member")
    slot_ids = jnp.arange(device_count, dtype=jnp.int32)
    dev_of_slot = (slot_ids % groups) * members + slot_ids // groups
    target_slot = (target_dev % members) * groups + target_dev // members
    picked = picked_dev[dev_of_slot]
    back_dest = back_dev[dev_of_slot]
    slot_pair = jnp.zeros((device_count,), jnp.int32).at[target_slot].set(
        jnp.arange(target_dev.shape[0], dtype=jnp.int32))
    slot_used = jnp.zeros((device_count,), jnp.int32).at[target_slot].set(1)
    h_order, h_starts = _lists(lhome, own_blocks)
    n_order, n_starts = _lists(lnear, own_blocks)
    r_order, r_starts = _lists(rhome, own_blocks)
    s_order, s_starts = _lists(back_dest, own_blocks)

    remote_tiles_t = jnp.swapaxes(remote_tiles, 1, 2)
    local_tiles_t = jnp.swapaxes(local_tiles, 1, 2)

    def apply_graph(blocks_in, init, extra=None):
        send = build_send(picked, slot_pair, slot_used, rhome, blocks_in, remote_tiles_t, extra)
        recv = lax.all_to_all(send, SLOT_AXES, split_axis=0, concat_axis=0, tiled=True)
        part = local_sum(h_starts, h_order, n_starts, n_order, lhome, lnear, blocks_in, local_tiles,
                         local_tiles_t, init)
        total = post_sum(r_starts, r_order, target_slot, s_starts, s_order, remote_tiles, recv, part)
        return total.reshape(row_count, F), recv

    zeros = jnp.zeros((own_blocks, BLOCK, F), jnp.float32)
    aggregate = apply_graph(features.reshape(own_blocks, BLOCK, F), zeros)[0].astype(jnp.bfloat16)
    joined = jnp.concatenate([features, aggregate], axis=1)
    pre_act = jnp.dot(joined, weight, preferred_element_type=jnp.float32)
    sigmoid_z = jax.nn.sigmoid(pre_act)
    output = (pre_act * sigmoid_z).astype(jnp.bfloat16)
    grad_pre = (
        cotangent.astype(jnp.float32) * sigmoid_z * (1.0 + pre_act * (1.0 - sigmoid_z))
    ).astype(jnp.bfloat16)
    partial_grad = jnp.einsum("ra,rf->af", joined, grad_pre, preferred_element_type=jnp.float32)
    rows = partial_grad.shape[0]
    chunk = rows // device_count
    pieces = partial_grad.reshape(device_count, chunk, F)[dev_of_slot]
    hi_f32 = lax.reduce_precision(pieces, exponent_bits=8, mantissa_bits=7)
    pieces_hi = hi_f32.astype(jnp.bfloat16)
    pieces_lo = (pieces - hi_f32).astype(jnp.bfloat16)
    extra = jnp.concatenate([pieces_hi, pieces_lo], axis=1)
    grad_joined = jnp.einsum("rf,af->ra", grad_pre, weight, preferred_element_type=jnp.float32)
    grad_agg = grad_joined[:, F:].astype(jnp.bfloat16).reshape(own_blocks, BLOCK, F)
    init_b = grad_joined[:, :F].reshape(own_blocks, BLOCK, F)
    grad_features, recv_b = apply_graph(grad_agg, init_b, extra)
    got = recv_b[:, 2 * BLOCK:, :].astype(jnp.float32)
    mine = jnp.sum(got[:, :chunk] + got[:, chunk:], axis=0)
    mine, grad_features = lax.optimization_barrier((mine, grad_features))
    grad_scale = 1.0 / math.sqrt(row_count * device_count)
    spread_out = jnp.broadcast_to(mine[None], (device_count, chunk, F))
    gathered = lax.all_to_all(spread_out, AXES, split_axis=0, concat_axis=0, tiled=True)
    grad_weight = gathered.reshape(rows, F) * grad_scale
    return (output, grad_weight, grad_features)


def solution(mesh):
    in_specs = (
        P(AXES, None),
        P(AXES),
        P(AXES),
        P(AXES, None, None),
        P(AXES),
        P(AXES),
        P(AXES, None, None),
        P(),
        P(AXES, None),
    )
    out_specs = (P(AXES, None), P(), P(AXES, None))
    return jax.shard_map(body, mesh=mesh, in_specs=in_specs, out_specs=out_specs, check_vma=False)
```

```python
import math

import jax
import jax.numpy as jnp
from jax import lax
from jax.experimental import pallas as pl
from jax.experimental.pallas import tpu as pltpu
from jax.sharding import PartitionSpec as P

F = 256
BLOCK = 128
BLK_DEV = 16
AXES = ("group", "member")
SLOT_AXES = ("member", "group")
VMEM_LIMIT = 56 * 1024 * 1024


def _smem():
    return pl.BlockSpec(memory_space=pltpu.SMEM)


def _vmem():
    return pl.BlockSpec(memory_space=pltpu.VMEM)


def _dot_t(a, v):
    return lax.dot_general(a, v, (((0,), (0,)), ((), ())), preferred_element_type=jnp.float32)


def _lists(dest, n_dest):
    order = jnp.argsort(dest, stable=True).astype(jnp.int32)
    counts = jnp.sum(dest[:, None] == jnp.arange(n_dest, dtype=jnp.int32)[None, :], axis=0)
    starts = jnp.concatenate([jnp.zeros((1,), jnp.int32), jnp.cumsum(counts).astype(jnp.int32)])
    return order, starts


def _pair_loop(lo, hi, term, acc):
    count = hi - lo
    iters = (count + 1) // 2

    def step(i, a):
        i0 = lo + 2 * i
        i1 = i0 + 1
        return a + term(i0, jnp.minimum(i1, hi - 1), i1 < hi)

    return lax.fori_loop(0, iters, step, acc)


def _local_kernel(hs_ref, ho_ref, ns_ref, no_ref, lh_ref, ln_ref, x_ref, lt_ref, init_ref, out_ref):
    blocks = out_ref.shape[0]

    def per_block(k, c):
        acc = init_ref[k]

        def home_term(i0, i1, ok):
            p0 = ho_ref[i0]
            p1 = ho_ref[i1]
            lhs = jnp.concatenate([lt_ref[p0], lt_ref[p1]], axis=1)
            v1 = jnp.where(ok, x_ref[ln_ref[p1]], jnp.zeros((BLOCK, F), x_ref.dtype))
            rhs = jnp.concatenate([x_ref[ln_ref[p0]], v1], axis=0)
            return jnp.dot(lhs, rhs, preferred_element_type=jnp.float32)

        acc = _pair_loop(hs_ref[k], hs_ref[k + 1], home_term, acc)

        def near_term(i0, i1, ok):
            p0 = no_ref[i0]
            p1 = no_ref[i1]
            lhs = jnp.concatenate([lt_ref[p0], lt_ref[p1]], axis=0)
            v1 = jnp.where(ok, x_ref[lh_ref[p1]], jnp.zeros((BLOCK, F), x_ref.dtype))
            rhs = jnp.concatenate([x_ref[lh_ref[p0]], v1], axis=0)
            return _dot_t(lhs, rhs)

        acc = _pair_loop(ns_ref[k], ns_ref[k + 1], near_term, acc)
        out_ref[k] = acc
        return c

    lax.fori_loop(0, blocks, per_block, 0)


def local_sum(hs, ho, ns, no, lh, ln, x, ltiles, init):
    pairs = ltiles.shape[0]
    cost = pl.CostEstimate(
        flops=2 * 2 * pairs * BLOCK * BLOCK * F,
        transcendentals=0,
        bytes_accessed=x.size * 2 + ltiles.size * 2 + init.size * 8,
    )
    return pl.pallas_call(
        _local_kernel,
        out_shape=jax.ShapeDtypeStruct(init.shape, jnp.float32),
        in_specs=[_smem()] * 6 + [_vmem()] * 3,
        out_specs=_vmem(),
        cost_estimate=cost,
        compiler_params=pltpu.CompilerParams(vmem_limit_bytes=VMEM_LIMIT),
    )(hs, ho, ns, no, lh, ln, x, ltiles, init)


SEND_GROUP = 8


def _send_kernel(picked_ref, spair_ref, sused_ref, rhome_ref, x_ref, rt_ref, *rest):
    send_ref = rest[-1]
    extra_ref = rest[0] if len(rest) == 2 and rest[0].shape[0] == send_ref.shape[0] else None
    base = pl.program_id(0) * SEND_GROUP
    for j in range(SEND_GROUP):
        t = base + j
        send_ref[j, pl.ds(0, BLOCK)] = x_ref[picked_ref[t]]
        p = spair_ref[t]
        r = _dot_t(rt_ref[p], x_ref[rhome_ref[p]])
        r = jnp.where(sused_ref[t] > 0, r, 0.0)
        send_ref[j, pl.ds(BLOCK, BLOCK)] = r.astype(send_ref.dtype)
        if extra_ref is not None:
            send_ref[j, pl.ds(2 * BLOCK, extra_ref.shape[1])] = extra_ref[j]


def build_send(picked, spair, sused, rhome, x, rtiles, extra=None, after=None):
    slots = picked.shape[0]
    full3 = lambda i: (0, 0, 0)
    extra_rows = 0 if extra is None else extra.shape[1]
    rows = 2 * BLOCK + extra_rows
    cost = pl.CostEstimate(
        flops=2 * slots * BLOCK * BLOCK * F,
        transcendentals=0,
        bytes_accessed=x.size * 2 + rtiles.size * 2 + slots * rows * F * 2,
    )
    in_specs = [_smem()] * 4 + [pl.BlockSpec(x.shape, full3), pl.BlockSpec(rtiles.shape, full3)]
    args = [picked, spair, sused, rhome, x, rtiles]
    if extra is not None:
        in_specs.append(pl.BlockSpec((SEND_GROUP, extra_rows, F), lambda i: (i, 0, 0)))
        args.append(extra)
    if after is not None:
        in_specs.append(pl.BlockSpec(memory_space=pl.ANY))
        args.append(after)
    return pl.pallas_call(
        _send_kernel,
        grid=(slots // SEND_GROUP,),
        out_shape=jax.ShapeDtypeStruct((slots, rows, F), jnp.bfloat16),
        in_specs=in_specs,
        out_specs=pl.BlockSpec((SEND_GROUP, rows, F), lambda i: (i, 0, 0)),
        cost_estimate=cost,
        compiler_params=pltpu.CompilerParams(vmem_limit_bytes=VMEM_LIMIT),
    )(*args)


def _post_kernel(rs_ref, ro_ref, td_ref, ss_ref, so_ref, rt_ref, recv_ref, base_ref, out_ref):
    blocks = out_ref.shape[0]

    def per_block(k, c):
        acc = base_ref[k]

        def remote_term(i0, i1, ok):
            p0 = ro_ref[i0]
            p1 = ro_ref[i1]
            lhs = jnp.concatenate([rt_ref[p0], rt_ref[p1]], axis=1)
            v1 = jnp.where(ok, recv_ref[td_ref[p1], pl.ds(0, BLOCK)], jnp.zeros((BLOCK, F), recv_ref.dtype))
            rhs = jnp.concatenate([recv_ref[td_ref[p0], pl.ds(0, BLOCK)], v1], axis=0)
            return jnp.dot(lhs, rhs, preferred_element_type=jnp.float32)

        acc = _pair_loop(rs_ref[k], rs_ref[k + 1], remote_term, acc)

        def back_term(i, a):
            return a + recv_ref[so_ref[i], pl.ds(BLOCK, BLOCK)].astype(jnp.float32)

        acc = lax.fori_loop(ss_ref[k], ss_ref[k + 1], back_term, acc)
        out_ref[k] = acc
        return c

    lax.fori_loop(0, blocks, per_block, 0)


def post_sum(rs, ro, td, ss, so, rtiles, recv, base):
    pairs = rtiles.shape[0]
    cost = pl.CostEstimate(
        flops=2 * pairs * BLOCK * BLOCK * F,
        transcendentals=0,
        bytes_accessed=rtiles.size * 2 + recv.size * 2 + base.size * 8,
    )
    return pl.pallas_call(
        _post_kernel,
        out_shape=jax.ShapeDtypeStruct(base.shape, jnp.float32),
        in_specs=[_smem()] * 5 + [_vmem()] * 3,
        out_specs=_vmem(),
        cost_estimate=cost,
        input_output_aliases={7: 0},
        compiler_params=pltpu.CompilerParams(vmem_limit_bytes=VMEM_LIMIT),
    )(rs, ro, td, ss, so, rtiles, recv, base)


def body(
    features,
    local_home,
    local_near,
    local_tiles,
    remote_home,
    remote_far,
    remote_tiles,
    weight,
    cotangent,
):
    device_count = lax.axis_size(AXES)
    row_count = features.shape[0]
    own_blocks = row_count // BLOCK
    lhome = jnp.clip(local_home, 0, own_blocks - 1)
    lnear = jnp.clip(local_near, 0, own_blocks - 1)
    rhome = jnp.clip(remote_home, 0, own_blocks - 1)
    target_dev = jnp.clip(remote_far // BLK_DEV, 0, device_count - 1)
    wanted = remote_far % BLK_DEV
    request = jnp.full((device_count,), -1, jnp.int32).at[target_dev].set(wanted)
    asked = lax.all_to_all(request, AXES, split_axis=0, concat_axis=0, tiled=True)
    picked_dev = jnp.clip(asked, 0, own_blocks - 1)
    back_dev = jnp.where(asked >= 0, picked_dev, own_blocks)
    groups = lax.axis_size("group")
    members = lax.axis_size("member")
    slot_ids = jnp.arange(device_count, dtype=jnp.int32)
    dev_of_slot = (slot_ids % groups) * members + slot_ids // groups
    target_slot = (target_dev % members) * groups + target_dev // members
    picked = picked_dev[dev_of_slot]
    back_dest = back_dev[dev_of_slot]
    slot_pair = jnp.zeros((device_count,), jnp.int32).at[target_slot].set(
        jnp.arange(target_dev.shape[0], dtype=jnp.int32))
    slot_used = jnp.zeros((device_count,), jnp.int32).at[target_slot].set(1)
    h_order, h_starts = _lists(lhome, own_blocks)
    n_order, n_starts = _lists(lnear, own_blocks)
    r_order, r_starts = _lists(rhome, own_blocks)
    s_order, s_starts = _lists(back_dest, own_blocks)

    def apply_graph(blocks_in, init, extra=None, local_first=False):
        part = local_sum(h_starts, h_order, n_starts, n_order, lhome, lnear, blocks_in, local_tiles, init)
        send = build_send(picked, slot_pair, slot_used, rhome, blocks_in, remote_tiles, extra,
                          part if local_first else None)
        recv = lax.all_to_all(send, SLOT_AXES, split_axis=0, concat_axis=0, tiled=True)
        total = post_sum(r_starts, r_order, target_slot, s_starts, s_order, remote_tiles, recv, part)
        return total.reshape(row_count, F), recv

    zeros = jnp.zeros((own_blocks, BLOCK, F), jnp.float32)
    aggregate = apply_graph(features.reshape(own_blocks, BLOCK, F), zeros, local_first=True)[0].astype(jnp.bfloat16)
    joined = jnp.concatenate([features, aggregate], axis=1)
    pre_act = jnp.dot(joined, weight, preferred_element_type=jnp.float32)
    sigmoid_z = jax.nn.sigmoid(pre_act)
    output = (pre_act * sigmoid_z).astype(jnp.bfloat16)
    grad_pre = (
        cotangent.astype(jnp.float32) * sigmoid_z * (1.0 + pre_act * (1.0 - sigmoid_z))
    ).astype(jnp.bfloat16)
    partial_grad = jnp.einsum("ra,rf->af", joined, grad_pre, preferred_element_type=jnp.float32)
    rows = partial_grad.shape[0]
    chunk = rows // device_count
    pieces = partial_grad.reshape(device_count, chunk, F)[dev_of_slot]
    hi_f32 = lax.reduce_precision(pieces, exponent_bits=8, mantissa_bits=7)
    pieces_hi = hi_f32.astype(jnp.bfloat16)
    pieces_lo = (pieces - hi_f32).astype(jnp.bfloat16)
    extra = jnp.concatenate([pieces_hi, pieces_lo], axis=1)
    grad_joined = jnp.einsum("rf,af->ra", grad_pre, weight, preferred_element_type=jnp.float32)
    grad_agg = grad_joined[:, F:].astype(jnp.bfloat16).reshape(own_blocks, BLOCK, F)
    init_b = grad_joined[:, :F].reshape(own_blocks, BLOCK, F)
    grad_features, recv_b = apply_graph(grad_agg, init_b, extra)
    got = recv_b[:, 2 * BLOCK:, :].astype(jnp.float32)
    mine = jnp.sum(got[:, :chunk] + got[:, chunk:], axis=0)
    mine, grad_features = lax.optimization_barrier((mine, grad_features))
    grad_scale = 1.0 / math.sqrt(row_count * device_count)
    spread_out = jnp.broadcast_to(mine[None], (device_count, chunk, F))
    gathered = lax.all_to_all(spread_out, AXES, split_axis=0, concat_axis=0, tiled=True)
    grad_weight = gathered.reshape(rows, F) * grad_scale
    return (output, grad_weight, grad_features)


def solution(mesh):
    in_specs = (
        P(AXES, None),
        P(AXES),
        P(AXES),
        P(AXES, None, None),
        P(AXES),
        P(AXES),
        P(AXES, None, None),
        P(),
        P(AXES, None),
    )
    out_specs = (P(AXES, None), P(), P(AXES, None))
    return jax.shard_map(body, mesh=mesh, in_specs=in_specs, out_specs=out_specs, check_vma=False)
```

```python
import math

import jax
import jax.numpy as jnp
from jax import lax
from jax.experimental import pallas as pl
from jax.experimental.pallas import tpu as pltpu
from jax.sharding import PartitionSpec as P

F = 256
BLOCK = 128
BLK_DEV = 16
AXES = ("group", "member")
SLOT_AXES = ("member", "group")
VMEM_LIMIT = 56 * 1024 * 1024


def _smem():
    return pl.BlockSpec(memory_space=pltpu.SMEM)


def _vmem():
    return pl.BlockSpec(memory_space=pltpu.VMEM)


def _dot_t(a, v):
    return lax.dot_general(a, v, (((0,), (0,)), ((), ())), preferred_element_type=jnp.float32)


def _lists(dest, n_dest):
    order = jnp.argsort(dest, stable=True).astype(jnp.int32)
    counts = jnp.sum(dest[:, None] == jnp.arange(n_dest, dtype=jnp.int32)[None, :], axis=0)
    starts = jnp.concatenate([jnp.zeros((1,), jnp.int32), jnp.cumsum(counts).astype(jnp.int32)])
    return order, starts


def _pair_loop(lo, hi, term, acc):
    count = hi - lo
    iters = (count + 1) // 2

    def step(i, a):
        i0 = lo + 2 * i
        i1 = i0 + 1
        return a + term(i0, jnp.minimum(i1, hi - 1), i1 < hi)

    return lax.fori_loop(0, iters, step, acc)


def _local_kernel(hs_ref, ho_ref, ns_ref, no_ref, lh_ref, ln_ref, x_ref, lt_ref, init_ref, out_ref):
    blocks = out_ref.shape[0]

    def per_block(k, c):
        acc = init_ref[k]

        def home_term(i0, i1, ok):
            p0 = ho_ref[i0]
            p1 = ho_ref[i1]
            lhs = jnp.concatenate([lt_ref[p0], lt_ref[p1]], axis=1)
            v1 = jnp.where(ok, x_ref[ln_ref[p1]], jnp.zeros((BLOCK, F), x_ref.dtype))
            rhs = jnp.concatenate([x_ref[ln_ref[p0]], v1], axis=0)
            return jnp.dot(lhs, rhs, preferred_element_type=jnp.float32)

        acc = _pair_loop(hs_ref[k], hs_ref[k + 1], home_term, acc)

        def near_term(i0, i1, ok):
            p0 = no_ref[i0]
            p1 = no_ref[i1]
            lhs = jnp.concatenate([lt_ref[p0], lt_ref[p1]], axis=0)
            v1 = jnp.where(ok, x_ref[lh_ref[p1]], jnp.zeros((BLOCK, F), x_ref.dtype))
            rhs = jnp.concatenate([x_ref[lh_ref[p0]], v1], axis=0)
            return _dot_t(lhs, rhs)

        acc = _pair_loop(ns_ref[k], ns_ref[k + 1], near_term, acc)
        out_ref[k] = acc
        return c

    lax.fori_loop(0, blocks, per_block, 0)


def local_sum(hs, ho, ns, no, lh, ln, x, ltiles, init):
    pairs = ltiles.shape[0]
    cost = pl.CostEstimate(
        flops=2 * 2 * pairs * BLOCK * BLOCK * F,
        transcendentals=0,
        bytes_accessed=x.size * 2 + ltiles.size * 2 + init.size * 8,
    )
    return pl.pallas_call(
        _local_kernel,
        out_shape=jax.ShapeDtypeStruct(init.shape, jnp.float32),
        in_specs=[_smem()] * 6 + [_vmem()] * 3,
        out_specs=_vmem(),
        cost_estimate=cost,
        compiler_params=pltpu.CompilerParams(vmem_limit_bytes=VMEM_LIMIT),
    )(hs, ho, ns, no, lh, ln, x, ltiles, init)


SEND_GROUP = 16


def _send_kernel(picked_ref, spair_ref, sused_ref, rhome_ref, x_ref, rt_ref, *rest):
    send_ref = rest[-1]
    extra_ref = rest[0] if len(rest) == 2 else None
    group = send_ref.shape[0]
    base = pl.program_id(0) * group
    for j in range(group):
        t = base + j
        send_ref[j, pl.ds(0, BLOCK)] = x_ref[picked_ref[t]]
        p = spair_ref[t]
        r = _dot_t(rt_ref[p], x_ref[rhome_ref[p]])
        r = jnp.where(sused_ref[t] > 0, r, 0.0)
        send_ref[j, pl.ds(BLOCK, BLOCK)] = r.astype(send_ref.dtype)
        if extra_ref is not None:
            send_ref[j, pl.ds(2 * BLOCK, extra_ref.shape[1])] = extra_ref[j]


def build_send(picked, spair, sused, rhome, x, rtiles, extra=None):
    slots = picked.shape[0]
    group = math.gcd(SEND_GROUP, slots)
    full3 = lambda i: (0, 0, 0)
    extra_rows = 0 if extra is None else extra.shape[1]
    rows = 2 * BLOCK + extra_rows
    cost = pl.CostEstimate(
        flops=2 * slots * BLOCK * BLOCK * F,
        transcendentals=0,
        bytes_accessed=x.size * 2 + rtiles.size * 2 + slots * rows * F * 2,
    )
    in_specs = [_smem()] * 4 + [pl.BlockSpec(x.shape, full3), pl.BlockSpec(rtiles.shape, full3)]
    args = [picked, spair, sused, rhome, x, rtiles]
    if extra is not None:
        in_specs.append(pl.BlockSpec((group, extra_rows, F), lambda i: (i, 0, 0)))
        args.append(extra)
    return pl.pallas_call(
        _send_kernel,
        grid=(slots // group,),
        out_shape=jax.ShapeDtypeStruct((slots, rows, F), jnp.bfloat16),
        in_specs=in_specs,
        out_specs=pl.BlockSpec((group, rows, F), lambda i: (i, 0, 0)),
        cost_estimate=cost,
        compiler_params=pltpu.CompilerParams(vmem_limit_bytes=VMEM_LIMIT),
    )(*args)


def _post_kernel(rs_ref, ro_ref, td_ref, ss_ref, so_ref, rt_ref, recv_ref, base_ref, out_ref):
    blocks = out_ref.shape[0]

    def per_block(k, c):
        acc = base_ref[k]

        def remote_term(i0, i1, ok):
            p0 = ro_ref[i0]
            p1 = ro_ref[i1]
            lhs = jnp.concatenate([rt_ref[p0], rt_ref[p1]], axis=1)
            v1 = jnp.where(ok, recv_ref[td_ref[p1], pl.ds(0, BLOCK)], jnp.zeros((BLOCK, F), recv_ref.dtype))
            rhs = jnp.concatenate([recv_ref[td_ref[p0], pl.ds(0, BLOCK)], v1], axis=0)
            return jnp.dot(lhs, rhs, preferred_element_type=jnp.float32)

        acc = _pair_loop(rs_ref[k], rs_ref[k + 1], remote_term, acc)

        def back_term(i, a):
            return a + recv_ref[so_ref[i], pl.ds(BLOCK, BLOCK)].astype(jnp.float32)

        acc = lax.fori_loop(ss_ref[k], ss_ref[k + 1], back_term, acc)
        out_ref[k] = acc
        return c

    lax.fori_loop(0, blocks, per_block, 0)


def post_sum(rs, ro, td, ss, so, rtiles, recv, base):
    pairs = rtiles.shape[0]
    cost = pl.CostEstimate(
        flops=2 * pairs * BLOCK * BLOCK * F,
        transcendentals=0,
        bytes_accessed=rtiles.size * 2 + recv.size * 2 + base.size * 8,
    )
    return pl.pallas_call(
        _post_kernel,
        out_shape=jax.ShapeDtypeStruct(base.shape, jnp.float32),
        in_specs=[_smem()] * 5 + [_vmem()] * 3,
        out_specs=_vmem(),
        cost_estimate=cost,
        input_output_aliases={7: 0},
        compiler_params=pltpu.CompilerParams(vmem_limit_bytes=VMEM_LIMIT),
    )(rs, ro, td, ss, so, rtiles, recv, base)


def body(
    features,
    local_home,
    local_near,
    local_tiles,
    remote_home,
    remote_far,
    remote_tiles,
    weight,
    cotangent,
):
    device_count = lax.axis_size(AXES)
    row_count = features.shape[0]
    own_blocks = row_count // BLOCK
    lhome = jnp.clip(local_home, 0, own_blocks - 1)
    lnear = jnp.clip(local_near, 0, own_blocks - 1)
    rhome = jnp.clip(remote_home, 0, own_blocks - 1)
    target_dev = jnp.clip(remote_far // BLK_DEV, 0, device_count - 1)
    wanted = remote_far % BLK_DEV
    request = jnp.full((device_count,), -1, jnp.int32).at[target_dev].set(wanted)
    asked = lax.all_to_all(request, AXES, split_axis=0, concat_axis=0, tiled=True)
    picked_dev = jnp.clip(asked, 0, own_blocks - 1)
    back_dev = jnp.where(asked >= 0, picked_dev, own_blocks)
    groups = lax.axis_size("group")
    members = lax.axis_size("member")
    slot_ids = jnp.arange(device_count, dtype=jnp.int32)
    dev_of_slot = (slot_ids % groups) * members + slot_ids // groups
    target_slot = (target_dev % members) * groups + target_dev // members
    picked = picked_dev[dev_of_slot]
    back_dest = back_dev[dev_of_slot]
    slot_pair = jnp.zeros((device_count,), jnp.int32).at[target_slot].set(
        jnp.arange(target_dev.shape[0], dtype=jnp.int32))
    slot_used = jnp.zeros((device_count,), jnp.int32).at[target_slot].set(1)
    h_order, h_starts = _lists(lhome, own_blocks)
    n_order, n_starts = _lists(lnear, own_blocks)
    r_order, r_starts = _lists(rhome, own_blocks)
    s_order, s_starts = _lists(back_dest, own_blocks)

    def apply_graph(blocks_in, init, extra=None):
        send = build_send(picked, slot_pair, slot_used, rhome, blocks_in, remote_tiles, extra)
        recv = lax.all_to_all(send, SLOT_AXES, split_axis=0, concat_axis=0, tiled=True)
        part = local_sum(h_starts, h_order, n_starts, n_order, lhome, lnear, blocks_in, local_tiles, init)
        total = post_sum(r_starts, r_order, target_slot, s_starts, s_order, remote_tiles, recv, part)
        return total.reshape(row_count, F), recv

    zeros = jnp.zeros((own_blocks, BLOCK, F), jnp.float32)
    aggregate = apply_graph(features.reshape(own_blocks, BLOCK, F), zeros)[0].astype(jnp.bfloat16)
    joined = jnp.concatenate([features, aggregate], axis=1)
    pre_act = jnp.dot(joined, weight, preferred_element_type=jnp.float32)
    sigmoid_z = jax.nn.sigmoid(pre_act)
    output = (pre_act * sigmoid_z).astype(jnp.bfloat16)
    grad_pre = (
        cotangent.astype(jnp.float32) * sigmoid_z * (1.0 + pre_act * (1.0 - sigmoid_z))
    ).astype(jnp.bfloat16)
    partial_grad = jnp.einsum("ra,rf->af", joined, grad_pre, preferred_element_type=jnp.float32)
    rows = partial_grad.shape[0]
    chunk = rows // device_count
    pieces = partial_grad.reshape(device_count, chunk, F)[dev_of_slot]
    hi_f32 = lax.reduce_precision(pieces, exponent_bits=8, mantissa_bits=7)
    pieces_hi = hi_f32.astype(jnp.bfloat16)
    pieces_lo = (pieces - hi_f32).astype(jnp.bfloat16)
    extra = jnp.concatenate([pieces_hi, pieces_lo], axis=1)
    grad_joined = jnp.einsum("rf,af->ra", grad_pre, weight, preferred_element_type=jnp.float32)
    grad_agg = grad_joined[:, F:].astype(jnp.bfloat16).reshape(own_blocks, BLOCK, F)
    init_b = grad_joined[:, :F].reshape(own_blocks, BLOCK, F)
    grad_features, recv_b = apply_graph(grad_agg, init_b, extra)
    got = recv_b[:, 2 * BLOCK:, :].astype(jnp.float32)
    mine = jnp.sum(got[:, :chunk] + got[:, chunk:], axis=0)
    mine, grad_features = lax.optimization_barrier((mine, grad_features))
    grad_scale = 1.0 / math.sqrt(row_count * device_count)
    spread_out = jnp.broadcast_to(mine[None], (device_count, chunk, F))
    gathered = lax.all_to_all(spread_out, AXES, split_axis=0, concat_axis=0, tiled=True)
    grad_weight = gathered.reshape(rows, F) * grad_scale
    return (output, grad_weight, grad_features)


def solution(mesh):
    in_specs = (
        P(AXES, None),
        P(AXES),
        P(AXES),
        P(AXES, None, None),
        P(AXES),
        P(AXES),
        P(AXES, None, None),
        P(),
        P(AXES, None),
    )
    out_specs = (P(AXES, None), P(), P(AXES, None))
    return jax.shard_map(body, mesh=mesh, in_specs=in_specs, out_specs=out_specs, check_vma=False)
```

```python
import math

import jax
import jax.numpy as jnp
from jax import lax
from jax.experimental import pallas as pl
from jax.experimental.pallas import tpu as pltpu
from jax.sharding import PartitionSpec as P

F = 256
BLOCK = 128
BLK_DEV = 16
AXES = ("group", "member")
SLOT_AXES = ("member", "group")
VMEM_LIMIT = 56 * 1024 * 1024


def _smem():
    return pl.BlockSpec(memory_space=pltpu.SMEM)


def _vmem():
    return pl.BlockSpec(memory_space=pltpu.VMEM)


def _dot_t(a, v):
    return lax.dot_general(a, v, (((0,), (0,)), ((), ())), preferred_element_type=jnp.float32)


def _lists(dest, n_dest):
    order = jnp.argsort(dest, stable=True).astype(jnp.int32)
    counts = jnp.sum(dest[:, None] == jnp.arange(n_dest, dtype=jnp.int32)[None, :], axis=0)
    starts = jnp.concatenate([jnp.zeros((1,), jnp.int32), jnp.cumsum(counts).astype(jnp.int32)])
    return order, starts


def _pair_loop(lo, hi, term, acc):
    count = hi - lo
    iters = (count + 1) // 2

    def step(i, a):
        i0 = lo + 2 * i
        i1 = i0 + 1
        return a + term(i0, jnp.minimum(i1, hi - 1), i1 < hi)

    return lax.fori_loop(0, iters, step, acc)


def _local_kernel(hs_ref, ho_ref, ns_ref, no_ref, lh_ref, ln_ref, x_ref, lt_ref, init_ref, out_ref):
    blocks = out_ref.shape[0]

    def per_block(k, c):
        acc = init_ref[k]

        def home_term(i0, i1, ok):
            p0 = ho_ref[i0]
            p1 = ho_ref[i1]
            lhs = jnp.concatenate([lt_ref[p0], lt_ref[p1]], axis=1)
            v1 = jnp.where(ok, x_ref[ln_ref[p1]], jnp.zeros((BLOCK, F), x_ref.dtype))
            rhs = jnp.concatenate([x_ref[ln_ref[p0]], v1], axis=0)
            return jnp.dot(lhs, rhs, preferred_element_type=jnp.float32)

        acc = _pair_loop(hs_ref[k], hs_ref[k + 1], home_term, acc)

        def near_term(i0, i1, ok):
            p0 = no_ref[i0]
            p1 = no_ref[i1]
            lhs = jnp.concatenate([lt_ref[p0], lt_ref[p1]], axis=0)
            v1 = jnp.where(ok, x_ref[lh_ref[p1]], jnp.zeros((BLOCK, F), x_ref.dtype))
            rhs = jnp.concatenate([x_ref[lh_ref[p0]], v1], axis=0)
            return _dot_t(lhs, rhs)

        acc = _pair_loop(ns_ref[k], ns_ref[k + 1], near_term, acc)
        out_ref[k] = acc
        return c

    lax.fori_loop(0, blocks, per_block, 0)


def local_sum(hs, ho, ns, no, lh, ln, x, ltiles, init):
    pairs = ltiles.shape[0]
    cost = pl.CostEstimate(
        flops=2 * 2 * pairs * BLOCK * BLOCK * F,
        transcendentals=0,
        bytes_accessed=x.size * 2 + ltiles.size * 2 + init.size * 8,
    )
    return pl.pallas_call(
        _local_kernel,
        out_shape=jax.ShapeDtypeStruct(init.shape, jnp.float32),
        in_specs=[_smem()] * 6 + [_vmem()] * 3,
        out_specs=_vmem(),
        cost_estimate=cost,
        compiler_params=pltpu.CompilerParams(vmem_limit_bytes=VMEM_LIMIT),
    )(hs, ho, ns, no, lh, ln, x, ltiles, init)


SEND_GROUP = 16


def _send_kernel(picked_ref, spair_ref, sused_ref, rhome_ref, x_ref, rt_ref, *rest):
    send_ref = rest[-1]
    extra_ref = rest[0] if len(rest) == 2 else None
    group = send_ref.shape[0]
    base = pl.program_id(0) * group
    for j in range(group):
        t = base + j
        send_ref[j, pl.ds(0, BLOCK)] = x_ref[picked_ref[t]]
        p = spair_ref[t]
        r = _dot_t(rt_ref[p], x_ref[rhome_ref[p]])
        r = jnp.where(sused_ref[t] > 0, r, 0.0)
        send_ref[j, pl.ds(BLOCK, BLOCK)] = r.astype(send_ref.dtype)
        if extra_ref is not None:
            send_ref[j, pl.ds(2 * BLOCK, extra_ref.shape[1])] = extra_ref[j]


def build_send(picked, spair, sused, rhome, x, rtiles, extra=None):
    slots = picked.shape[0]
    group = math.gcd(SEND_GROUP, slots)
    full3 = lambda i: (0, 0, 0)
    extra_rows = 0 if extra is None else extra.shape[1]
    rows = 2 * BLOCK + extra_rows
    cost = pl.CostEstimate(
        flops=2 * slots * BLOCK * BLOCK * F,
        transcendentals=0,
        bytes_accessed=x.size * 2 + rtiles.size * 2 + slots * rows * F * 2,
    )
    in_specs = [_smem()] * 4 + [pl.BlockSpec(x.shape, full3), pl.BlockSpec(rtiles.shape, full3)]
    args = [picked, spair, sused, rhome, x, rtiles]
    if extra is not None:
        in_specs.append(pl.BlockSpec((group, extra_rows, F), lambda i: (i, 0, 0)))
        args.append(extra)
    return pl.pallas_call(
        _send_kernel,
        grid=(slots // group,),
        out_shape=jax.ShapeDtypeStruct((slots, rows, F), jnp.bfloat16),
        in_specs=in_specs,
        out_specs=pl.BlockSpec((group, rows, F), lambda i: (i, 0, 0)),
        cost_estimate=cost,
        compiler_params=pltpu.CompilerParams(vmem_limit_bytes=VMEM_LIMIT),
    )(*args)


def _post_kernel(rs_ref, ro_ref, td_ref, ss_ref, so_ref, rt_ref, recv_ref, base_ref, out_ref):
    blocks = out_ref.shape[0]

    def per_block(k, c):
        acc = base_ref[k]

        def remote_term(i0, i1, ok):
            p0 = ro_ref[i0]
            p1 = ro_ref[i1]
            lhs = jnp.concatenate([rt_ref[p0], rt_ref[p1]], axis=1)
            v1 = jnp.where(ok, recv_ref[td_ref[p1], pl.ds(0, BLOCK)], jnp.zeros((BLOCK, F), recv_ref.dtype))
            rhs = jnp.concatenate([recv_ref[td_ref[p0], pl.ds(0, BLOCK)], v1], axis=0)
            return jnp.dot(lhs, rhs, preferred_element_type=jnp.float32)

        acc = _pair_loop(rs_ref[k], rs_ref[k + 1], remote_term, acc)

        def back_term(i, a):
            return a + recv_ref[so_ref[i], pl.ds(BLOCK, BLOCK)].astype(jnp.float32)

        acc = lax.fori_loop(ss_ref[k], ss_ref[k + 1], back_term, acc)
        out_ref[k] = acc
        return c

    lax.fori_loop(0, blocks, per_block, 0)


def post_sum(rs, ro, td, ss, so, rtiles, recv, base):
    pairs = rtiles.shape[0]
    cost = pl.CostEstimate(
        flops=2 * pairs * BLOCK * BLOCK * F,
        transcendentals=0,
        bytes_accessed=rtiles.size * 2 + recv.size * 2 + base.size * 8,
    )
    return pl.pallas_call(
        _post_kernel,
        out_shape=jax.ShapeDtypeStruct(base.shape, jnp.float32),
        in_specs=[_smem()] * 5 + [_vmem()] * 3,
        out_specs=_vmem(),
        cost_estimate=cost,
        input_output_aliases={7: 0},
        compiler_params=pltpu.CompilerParams(vmem_limit_bytes=VMEM_LIMIT),
    )(rs, ro, td, ss, so, rtiles, recv, base)


def body(
    features,
    local_home,
    local_near,
    local_tiles,
    remote_home,
    remote_far,
    remote_tiles,
    weight,
    cotangent,
):
    device_count = lax.axis_size(AXES)
    row_count = features.shape[0]
    own_blocks = row_count // BLOCK
    lhome = jnp.clip(local_home, 0, own_blocks - 1)
    lnear = jnp.clip(local_near, 0, own_blocks - 1)
    rhome = jnp.clip(remote_home, 0, own_blocks - 1)
    target_dev = jnp.clip(remote_far // BLK_DEV, 0, device_count - 1)
    wanted = remote_far % BLK_DEV
    request = jnp.full((device_count,), -1, jnp.int32).at[target_dev].set(wanted)
    asked = lax.all_to_all(request, AXES, split_axis=0, concat_axis=0, tiled=True)
    picked_dev = jnp.clip(asked, 0, own_blocks - 1)
    back_dev = jnp.where(asked >= 0, picked_dev, own_blocks)
    groups = lax.axis_size("group")
    members = lax.axis_size("member")
    slot_ids = jnp.arange(device_count, dtype=jnp.int32)
    dev_of_slot = (slot_ids % groups) * members + slot_ids // groups
    target_slot = (target_dev % members) * groups + target_dev // members
    picked = picked_dev[dev_of_slot]
    back_dest = back_dev[dev_of_slot]
    slot_pair = jnp.zeros((device_count,), jnp.int32).at[target_slot].set(
        jnp.arange(target_dev.shape[0], dtype=jnp.int32))
    slot_used = jnp.zeros((device_count,), jnp.int32).at[target_slot].set(1)
    h_order, h_starts = _lists(lhome, own_blocks)
    n_order, n_starts = _lists(lnear, own_blocks)
    r_order, r_starts = _lists(rhome, own_blocks)
    s_order, s_starts = _lists(back_dest, own_blocks)

    def apply_graph(blocks_in, init, extra=None):
        send = build_send(picked, slot_pair, slot_used, rhome, blocks_in, remote_tiles, extra)
        recv = lax.all_to_all(send, SLOT_AXES, split_axis=0, concat_axis=0, tiled=True)
        part = local_sum(h_starts, h_order, n_starts, n_order, lhome, lnear, blocks_in, local_tiles, init)
        total = post_sum(r_starts, r_order, target_slot, s_starts, s_order, remote_tiles, recv, part)
        return total.reshape(row_count, F), recv

    zeros = jnp.zeros((own_blocks, BLOCK, F), jnp.float32)
    aggregate = apply_graph(features.reshape(own_blocks, BLOCK, F), zeros)[0].astype(jnp.bfloat16)
    joined = jnp.concatenate([features, aggregate], axis=1)
    pre_act = jnp.dot(joined, weight, preferred_element_type=jnp.float32)
    sigmoid_z = jax.nn.sigmoid(pre_act)
    output = (pre_act * sigmoid_z).astype(jnp.bfloat16)
    grad_pre = (
        cotangent.astype(jnp.float32) * sigmoid_z * (1.0 + pre_act * (1.0 - sigmoid_z))
    ).astype(jnp.bfloat16)
    partial_grad = jnp.einsum("ra,rf->af", joined, grad_pre, preferred_element_type=jnp.float32)
    rows = partial_grad.shape[0]
    chunk = rows // device_count
    pieces = partial_grad.reshape(device_count, chunk, F)[dev_of_slot]
    hi_f32 = lax.reduce_precision(pieces, exponent_bits=8, mantissa_bits=7)
    pieces_hi = hi_f32.astype(jnp.bfloat16)
    pieces_lo = (pieces - hi_f32).astype(jnp.bfloat16)
    extra = jnp.concatenate([pieces_hi, pieces_lo], axis=1)
    grad_self = jnp.einsum("rf,af->ra", grad_pre, weight[:F], preferred_element_type=jnp.float32)
    grad_nbr = jnp.einsum("rf,af->ra", grad_pre, weight[F:], preferred_element_type=jnp.float32)
    grad_agg = grad_nbr.astype(jnp.bfloat16).reshape(own_blocks, BLOCK, F)
    init_b = grad_self.reshape(own_blocks, BLOCK, F)
    grad_features, recv_b = apply_graph(grad_agg, init_b, extra)
    got = recv_b[:, 2 * BLOCK:, :].astype(jnp.float32)
    mine = jnp.sum(got[:, :chunk] + got[:, chunk:], axis=0)
    mine, grad_features = lax.optimization_barrier((mine, grad_features))
    grad_scale = 1.0 / math.sqrt(row_count * device_count)
    spread_out = jnp.broadcast_to(mine[None], (device_count, chunk, F))
    gathered = lax.all_to_all(spread_out, AXES, split_axis=0, concat_axis=0, tiled=True)
    grad_weight = gathered.reshape(rows, F) * grad_scale
    return (output, grad_weight, grad_features)


def solution(mesh):
    in_specs = (
        P(AXES, None),
        P(AXES),
        P(AXES),
        P(AXES, None, None),
        P(AXES),
        P(AXES),
        P(AXES, None, None),
        P(),
        P(AXES, None),
    )
    out_specs = (P(AXES, None), P(), P(AXES, None))
    return jax.shard_map(body, mesh=mesh, in_specs=in_specs, out_specs=out_specs, check_vma=False)
```

```python
import math

import jax
import jax.numpy as jnp
from jax import lax
from jax.experimental import pallas as pl
from jax.experimental.pallas import tpu as pltpu
from jax.sharding import PartitionSpec as P

F = 256
BLOCK = 128
BLK_DEV = 16
AXES = ("group", "member")
SLOT_AXES = ("member", "group")
VMEM_LIMIT = 56 * 1024 * 1024


def _smem():
    return pl.BlockSpec(memory_space=pltpu.SMEM)


def _vmem():
    return pl.BlockSpec(memory_space=pltpu.VMEM)


def _dot_t(a, v):
    return lax.dot_general(a, v, (((0,), (0,)), ((), ())), preferred_element_type=jnp.float32)


def _lists(dest, n_dest):
    order = jnp.argsort(dest, stable=True).astype(jnp.int32)
    counts = jnp.sum(dest[:, None] == jnp.arange(n_dest, dtype=jnp.int32)[None, :], axis=0)
    starts = jnp.concatenate([jnp.zeros((1,), jnp.int32), jnp.cumsum(counts).astype(jnp.int32)])
    return order, starts


def _pair_loop(lo, hi, term, acc):
    count = hi - lo
    iters = (count + 1) // 2

    def step(i, a):
        i0 = lo + 2 * i
        i1 = i0 + 1
        return a + term(i0, jnp.minimum(i1, hi - 1), i1 < hi)

    return lax.fori_loop(0, iters, step, acc)


def _local_kernel(hs_ref, ho_ref, ns_ref, no_ref, lh_ref, ln_ref, x_ref, lt_ref, init_ref, out_ref):
    blocks = out_ref.shape[0]

    def per_block(k, c):
        acc = init_ref[k]

        def home_term(i0, i1, ok):
            p0 = ho_ref[i0]
            p1 = ho_ref[i1]
            lhs = jnp.concatenate([lt_ref[p0], lt_ref[p1]], axis=1)
            v1 = jnp.where(ok, x_ref[ln_ref[p1]], jnp.zeros((BLOCK, F), x_ref.dtype))
            rhs = jnp.concatenate([x_ref[ln_ref[p0]], v1], axis=0)
            return jnp.dot(lhs, rhs, preferred_element_type=jnp.float32)

        acc = _pair_loop(hs_ref[k], hs_ref[k + 1], home_term, acc)

        def near_term(i0, i1, ok):
            p0 = no_ref[i0]
            p1 = no_ref[i1]
            lhs = jnp.concatenate([lt_ref[p0], lt_ref[p1]], axis=0)
            v1 = jnp.where(ok, x_ref[lh_ref[p1]], jnp.zeros((BLOCK, F), x_ref.dtype))
            rhs = jnp.concatenate([x_ref[lh_ref[p0]], v1], axis=0)
            return _dot_t(lhs, rhs)

        acc = _pair_loop(ns_ref[k], ns_ref[k + 1], near_term, acc)
        out_ref[k] = acc
        return c

    lax.fori_loop(0, blocks, per_block, 0)


def local_sum(hs, ho, ns, no, lh, ln, x, ltiles, init):
    pairs = ltiles.shape[0]
    cost = pl.CostEstimate(
        flops=2 * 2 * pairs * BLOCK * BLOCK * F,
        transcendentals=0,
        bytes_accessed=x.size * 2 + ltiles.size * 2 + init.size * 8,
    )
    return pl.pallas_call(
        _local_kernel,
        out_shape=jax.ShapeDtypeStruct(init.shape, jnp.float32),
        in_specs=[_smem()] * 6 + [_vmem()] * 3,
        out_specs=_vmem(),
        cost_estimate=cost,
        compiler_params=pltpu.CompilerParams(vmem_limit_bytes=VMEM_LIMIT),
    )(hs, ho, ns, no, lh, ln, x, ltiles, init)


SEND_GROUP = 16


def _send_kernel(picked_ref, spair_ref, sused_ref, rhome_ref, x_ref, rt_ref, *rest):
    send_ref = rest[-1]
    extra_ref = rest[0] if len(rest) == 2 else None
    group = send_ref.shape[0]
    base = pl.program_id(0) * group
    for j in range(group):
        t = base + j
        send_ref[j, pl.ds(0, BLOCK)] = x_ref[picked_ref[t]]
        p = spair_ref[t]
        r = _dot_t(rt_ref[p], x_ref[rhome_ref[p]])
        r = jnp.where(sused_ref[t] > 0, r, 0.0)
        send_ref[j, pl.ds(BLOCK, BLOCK)] = r.astype(send_ref.dtype)
        if extra_ref is not None:
            send_ref[j, pl.ds(2 * BLOCK, extra_ref.shape[1])] = extra_ref[j]


def build_send(picked, spair, sused, rhome, x, rtiles, extra=None):
    slots = picked.shape[0]
    group = math.gcd(SEND_GROUP, slots)
    full3 = lambda i: (0, 0, 0)
    extra_rows = 0 if extra is None else extra.shape[1]
    rows = 2 * BLOCK + extra_rows
    cost = pl.CostEstimate(
        flops=2 * slots * BLOCK * BLOCK * F,
        transcendentals=0,
        bytes_accessed=x.size * 2 + rtiles.size * 2 + slots * rows * F * 2,
    )
    in_specs = [_smem()] * 4 + [pl.BlockSpec(x.shape, full3), pl.BlockSpec(rtiles.shape, full3)]
    args = [picked, spair, sused, rhome, x, rtiles]
    if extra is not None:
        in_specs.append(pl.BlockSpec((group, extra_rows, F), lambda i: (i, 0, 0)))
        args.append(extra)
    return pl.pallas_call(
        _send_kernel,
        grid=(slots // group,),
        out_shape=jax.ShapeDtypeStruct((slots, rows, F), jnp.bfloat16),
        in_specs=in_specs,
        out_specs=pl.BlockSpec((group, rows, F), lambda i: (i, 0, 0)),
        cost_estimate=cost,
        compiler_params=pltpu.CompilerParams(vmem_limit_bytes=VMEM_LIMIT),
    )(*args)


def _post_kernel(rs_ref, ro_ref, td_ref, ss_ref, so_ref, rt_ref, recv_ref, base_ref, out_ref):
    blocks = out_ref.shape[0]

    def per_block(k, c):
        acc = base_ref[k]

        def remote_term(i0, i1, ok):
            p0 = ro_ref[i0]
            p1 = ro_ref[i1]
            lhs = jnp.concatenate([rt_ref[p0], rt_ref[p1]], axis=1)
            v1 = jnp.where(ok, recv_ref[td_ref[p1], pl.ds(0, BLOCK)], jnp.zeros((BLOCK, F), recv_ref.dtype))
            rhs = jnp.concatenate([recv_ref[td_ref[p0], pl.ds(0, BLOCK)], v1], axis=0)
            return jnp.dot(lhs, rhs, preferred_element_type=jnp.float32)

        acc = _pair_loop(rs_ref[k], rs_ref[k + 1], remote_term, acc)

        def back_term(i, a):
            return a + recv_ref[so_ref[i], pl.ds(BLOCK, BLOCK)].astype(jnp.float32)

        acc = lax.fori_loop(ss_ref[k], ss_ref[k + 1], back_term, acc)
        out_ref[k] = acc.astype(out_ref.dtype)
        return c

    lax.fori_loop(0, blocks, per_block, 0)


def post_sum(rs, ro, td, ss, so, rtiles, recv, base, out_dtype=jnp.float32):
    pairs = rtiles.shape[0]
    cost = pl.CostEstimate(
        flops=2 * pairs * BLOCK * BLOCK * F,
        transcendentals=0,
        bytes_accessed=rtiles.size * 2 + recv.size * 2 + base.size * 8,
    )
    return pl.pallas_call(
        _post_kernel,
        out_shape=jax.ShapeDtypeStruct(base.shape, out_dtype),
        in_specs=[_smem()] * 5 + [_vmem()] * 3,
        out_specs=_vmem(),
        cost_estimate=cost,
        input_output_aliases={7: 0} if out_dtype == base.dtype else {},
        compiler_params=pltpu.CompilerParams(vmem_limit_bytes=VMEM_LIMIT),
    )(rs, ro, td, ss, so, rtiles, recv, base)


def body(
    features,
    local_home,
    local_near,
    local_tiles,
    remote_home,
    remote_far,
    remote_tiles,
    weight,
    cotangent,
):
    device_count = lax.axis_size(AXES)
    row_count = features.shape[0]
    own_blocks = row_count // BLOCK
    lhome = jnp.clip(local_home, 0, own_blocks - 1)
    lnear = jnp.clip(local_near, 0, own_blocks - 1)
    rhome = jnp.clip(remote_home, 0, own_blocks - 1)
    target_dev = jnp.clip(remote_far // BLK_DEV, 0, device_count - 1)
    wanted = remote_far % BLK_DEV
    request = jnp.full((device_count,), -1, jnp.int32).at[target_dev].set(wanted)
    asked = lax.all_to_all(request, AXES, split_axis=0, concat_axis=0, tiled=True)
    picked_dev = jnp.clip(asked, 0, own_blocks - 1)
    back_dev = jnp.where(asked >= 0, picked_dev, own_blocks)
    groups = lax.axis_size("group")
    members = lax.axis_size("member")
    slot_ids = jnp.arange(device_count, dtype=jnp.int32)
    dev_of_slot = (slot_ids % groups) * members + slot_ids // groups
    target_slot = (target_dev % members) * groups + target_dev // members
    picked = picked_dev[dev_of_slot]
    back_dest = back_dev[dev_of_slot]
    slot_pair = jnp.zeros((device_count,), jnp.int32).at[target_slot].set(
        jnp.arange(target_dev.shape[0], dtype=jnp.int32))
    slot_used = jnp.zeros((device_count,), jnp.int32).at[target_slot].set(1)
    h_order, h_starts = _lists(lhome, own_blocks)
    n_order, n_starts = _lists(lnear, own_blocks)
    r_order, r_starts = _lists(rhome, own_blocks)
    s_order, s_starts = _lists(back_dest, own_blocks)

    def apply_graph(blocks_in, init, extra=None, out_dtype=jnp.float32):
        send = build_send(picked, slot_pair, slot_used, rhome, blocks_in, remote_tiles, extra)
        recv = lax.all_to_all(send, SLOT_AXES, split_axis=0, concat_axis=0, tiled=True)
        part = local_sum(h_starts, h_order, n_starts, n_order, lhome, lnear, blocks_in, local_tiles, init)
        total = post_sum(r_starts, r_order, target_slot, s_starts, s_order, remote_tiles, recv, part,
                         out_dtype)
        return total.reshape(row_count, F), recv

    zeros = jnp.zeros((own_blocks, BLOCK, F), jnp.float32)
    aggregate = apply_graph(features.reshape(own_blocks, BLOCK, F), zeros, out_dtype=jnp.bfloat16)[0]
    joined = jnp.concatenate([features, aggregate], axis=1)
    pre_act = jnp.dot(joined, weight, preferred_element_type=jnp.float32)
    sigmoid_z = jax.nn.sigmoid(pre_act)
    output = (pre_act * sigmoid_z).astype(jnp.bfloat16)
    grad_pre = (
        cotangent.astype(jnp.float32) * sigmoid_z * (1.0 + pre_act * (1.0 - sigmoid_z))
    ).astype(jnp.bfloat16)
    partial_grad = jnp.einsum("ra,rf->af", joined, grad_pre, preferred_element_type=jnp.float32)
    rows = partial_grad.shape[0]
    chunk = rows // device_count
    pieces = partial_grad.reshape(device_count, chunk, F)[dev_of_slot]
    hi_f32 = lax.reduce_precision(pieces, exponent_bits=8, mantissa_bits=7)
    pieces_hi = hi_f32.astype(jnp.bfloat16)
    pieces_lo = (pieces - hi_f32).astype(jnp.bfloat16)
    extra = jnp.concatenate([pieces_hi, pieces_lo], axis=1)
    grad_self = jnp.einsum("rf,af->ra", grad_pre, weight[:F], preferred_element_type=jnp.float32)
    grad_nbr = jnp.einsum("rf,af->ra", grad_pre, weight[F:], preferred_element_type=jnp.float32)
    grad_agg = grad_nbr.astype(jnp.bfloat16).reshape(own_blocks, BLOCK, F)
    init_b = grad_self.reshape(own_blocks, BLOCK, F)
    grad_features, recv_b = apply_graph(grad_agg, init_b, extra)
    got = recv_b[:, 2 * BLOCK:, :].astype(jnp.float32)
    mine = jnp.sum(got[:, :chunk] + got[:, chunk:], axis=0)
    mine, grad_features = lax.optimization_barrier((mine, grad_features))
    grad_scale = 1.0 / math.sqrt(row_count * device_count)
    spread_out = jnp.broadcast_to(mine[None], (device_count, chunk, F))
    gathered = lax.all_to_all(spread_out, AXES, split_axis=0, concat_axis=0, tiled=True)
    grad_weight = gathered.reshape(rows, F) * grad_scale
    return (output, grad_weight, grad_features)


def solution(mesh):
    in_specs = (
        P(AXES, None),
        P(AXES),
        P(AXES),
        P(AXES, None, None),
        P(AXES),
        P(AXES),
        P(AXES, None, None),
        P(),
        P(AXES, None),
    )
    out_specs = (P(AXES, None), P(), P(AXES, None))
    return jax.shard_map(body, mesh=mesh, in_specs=in_specs, out_specs=out_specs, check_vma=False)
```

```python
import math

import jax
import jax.numpy as jnp
from jax import lax
from jax.experimental import pallas as pl
from jax.experimental.pallas import tpu as pltpu
from jax.sharding import PartitionSpec as P

F = 256
BLOCK = 128
BLK_DEV = 16
AXES = ("group", "member")
SLOT_AXES = ("member", "group")
VMEM_LIMIT = 56 * 1024 * 1024


def _smem():
    return pl.BlockSpec(memory_space=pltpu.SMEM)


def _vmem():
    return pl.BlockSpec(memory_space=pltpu.VMEM)


def _dot_t(a, v):
    return lax.dot_general(a, v, (((0,), (0,)), ((), ())), preferred_element_type=jnp.float32)


def _lists(dest, n_dest):
    order = jnp.argsort(dest, stable=True).astype(jnp.int32)
    counts = jnp.sum(dest[:, None] == jnp.arange(n_dest, dtype=jnp.int32)[None, :], axis=0)
    starts = jnp.concatenate([jnp.zeros((1,), jnp.int32), jnp.cumsum(counts).astype(jnp.int32)])
    return order, starts


def _pair_loop(lo, hi, term, acc):
    count = hi - lo
    iters = (count + 1) // 2

    def step(i, a):
        i0 = lo + 2 * i
        i1 = i0 + 1
        return a + term(i0, jnp.minimum(i1, hi - 1), i1 < hi)

    return lax.fori_loop(0, iters, step, acc)


def _local_kernel(hs_ref, ho_ref, ns_ref, no_ref, lh_ref, ln_ref, x_ref, lt_ref, init_ref, out_ref):
    blocks = out_ref.shape[0]

    def per_block(k, c):
        acc = init_ref[k]

        def home_term(i0, i1, ok):
            p0 = ho_ref[i0]
            p1 = ho_ref[i1]
            lhs = jnp.concatenate([lt_ref[p0], lt_ref[p1]], axis=1)
            v1 = jnp.where(ok, x_ref[ln_ref[p1]], jnp.zeros((BLOCK, F), x_ref.dtype))
            rhs = jnp.concatenate([x_ref[ln_ref[p0]], v1], axis=0)
            return jnp.dot(lhs, rhs, preferred_element_type=jnp.float32)

        acc = _pair_loop(hs_ref[k], hs_ref[k + 1], home_term, acc)

        def near_term(i0, i1, ok):
            p0 = no_ref[i0]
            p1 = no_ref[i1]
            lhs = jnp.concatenate([lt_ref[p0], lt_ref[p1]], axis=0)
            v1 = jnp.where(ok, x_ref[lh_ref[p1]], jnp.zeros((BLOCK, F), x_ref.dtype))
            rhs = jnp.concatenate([x_ref[lh_ref[p0]], v1], axis=0)
            return _dot_t(lhs, rhs)

        acc = _pair_loop(ns_ref[k], ns_ref[k + 1], near_term, acc)
        out_ref[k] = acc
        return c

    lax.fori_loop(0, blocks, per_block, 0)


def local_sum(hs, ho, ns, no, lh, ln, x, ltiles, init):
    pairs = ltiles.shape[0]
    cost = pl.CostEstimate(
        flops=2 * 2 * pairs * BLOCK * BLOCK * F,
        transcendentals=0,
        bytes_accessed=x.size * 2 + ltiles.size * 2 + init.size * 8,
    )
    return pl.pallas_call(
        _local_kernel,
        out_shape=jax.ShapeDtypeStruct(init.shape, jnp.float32),
        in_specs=[_smem()] * 6 + [_vmem()] * 3,
        out_specs=_vmem(),
        cost_estimate=cost,
        compiler_params=pltpu.CompilerParams(vmem_limit_bytes=VMEM_LIMIT),
    )(hs, ho, ns, no, lh, ln, x, ltiles, init)


SEND_GROUP = 32


def _send_kernel(picked_ref, spair_ref, sused_ref, rhome_ref, x_ref, rt_ref, *rest):
    send_ref = rest[-1]
    extra_ref = rest[0] if len(rest) == 2 else None
    group = send_ref.shape[0]
    base = pl.program_id(0) * group
    for j in range(group):
        t = base + j
        send_ref[j, pl.ds(0, BLOCK)] = x_ref[picked_ref[t]]
        p = spair_ref[t]
        r = _dot_t(rt_ref[p], x_ref[rhome_ref[p]])
        r = jnp.where(sused_ref[t] > 0, r, 0.0)
        send_ref[j, pl.ds(BLOCK, BLOCK)] = r.astype(send_ref.dtype)
        if extra_ref is not None:
            send_ref[j, pl.ds(2 * BLOCK, extra_ref.shape[1])] = extra_ref[j]


def build_send(picked, spair, sused, rhome, x, rtiles, extra=None):
    slots = picked.shape[0]
    group = math.gcd(SEND_GROUP, slots)
    full3 = lambda i: (0, 0, 0)
    extra_rows = 0 if extra is None else extra.shape[1]
    rows = 2 * BLOCK + extra_rows
    cost = pl.CostEstimate(
        flops=2 * slots * BLOCK * BLOCK * F,
        transcendentals=0,
        bytes_accessed=x.size * 2 + rtiles.size * 2 + slots * rows * F * 2,
    )
    in_specs = [_smem()] * 4 + [pl.BlockSpec(x.shape, full3), pl.BlockSpec(rtiles.shape, full3)]
    args = [picked, spair, sused, rhome, x, rtiles]
    if extra is not None:
        in_specs.append(pl.BlockSpec((group, extra_rows, F), lambda i: (i, 0, 0)))
        args.append(extra)
    return pl.pallas_call(
        _send_kernel,
        grid=(slots // group,),
        out_shape=jax.ShapeDtypeStruct((slots, rows, F), jnp.bfloat16),
        in_specs=in_specs,
        out_specs=pl.BlockSpec((group, rows, F), lambda i: (i, 0, 0)),
        cost_estimate=cost,
        compiler_params=pltpu.CompilerParams(vmem_limit_bytes=VMEM_LIMIT),
    )(*args)


def _post_kernel(rs_ref, ro_ref, td_ref, ss_ref, so_ref, rt_ref, recv_ref, base_ref, out_ref):
    blocks = out_ref.shape[0]

    def per_block(k, c):
        acc = base_ref[k]

        def remote_term(i0, i1, ok):
            p0 = ro_ref[i0]
            p1 = ro_ref[i1]
            lhs = jnp.concatenate([rt_ref[p0], rt_ref[p1]], axis=1)
            v1 = jnp.where(ok, recv_ref[td_ref[p1], pl.ds(0, BLOCK)], jnp.zeros((BLOCK, F), recv_ref.dtype))
            rhs = jnp.concatenate([recv_ref[td_ref[p0], pl.ds(0, BLOCK)], v1], axis=0)
            return jnp.dot(lhs, rhs, preferred_element_type=jnp.float32)

        acc = _pair_loop(rs_ref[k], rs_ref[k + 1], remote_term, acc)

        def back_term(i, a):
            return a + recv_ref[so_ref[i], pl.ds(BLOCK, BLOCK)].astype(jnp.float32)

        acc = lax.fori_loop(ss_ref[k], ss_ref[k + 1], back_term, acc)
        out_ref[k] = acc.astype(out_ref.dtype)
        return c

    lax.fori_loop(0, blocks, per_block, 0)


def post_sum(rs, ro, td, ss, so, rtiles, recv, base, out_dtype=jnp.float32):
    pairs = rtiles.shape[0]
    cost = pl.CostEstimate(
        flops=2 * pairs * BLOCK * BLOCK * F,
        transcendentals=0,
        bytes_accessed=rtiles.size * 2 + recv.size * 2 + base.size * 8,
    )
    return pl.pallas_call(
        _post_kernel,
        out_shape=jax.ShapeDtypeStruct(base.shape, out_dtype),
        in_specs=[_smem()] * 5 + [_vmem()] * 3,
        out_specs=_vmem(),
        cost_estimate=cost,
        input_output_aliases={7: 0} if out_dtype == base.dtype else {},
        compiler_params=pltpu.CompilerParams(vmem_limit_bytes=VMEM_LIMIT),
    )(rs, ro, td, ss, so, rtiles, recv, base)


def body(
    features,
    local_home,
    local_near,
    local_tiles,
    remote_home,
    remote_far,
    remote_tiles,
    weight,
    cotangent,
):
    device_count = lax.axis_size(AXES)
    row_count = features.shape[0]
    own_blocks = row_count // BLOCK
    lhome = jnp.clip(local_home, 0, own_blocks - 1)
    lnear = jnp.clip(local_near, 0, own_blocks - 1)
    rhome = jnp.clip(remote_home, 0, own_blocks - 1)
    target_dev = jnp.clip(remote_far // BLK_DEV, 0, device_count - 1)
    wanted = remote_far % BLK_DEV
    request = jnp.full((device_count,), -1, jnp.int32).at[target_dev].set(wanted)
    asked = lax.all_to_all(request, AXES, split_axis=0, concat_axis=0, tiled=True)
    picked_dev = jnp.clip(asked, 0, own_blocks - 1)
    back_dev = jnp.where(asked >= 0, picked_dev, own_blocks)
    groups = lax.axis_size("group")
    members = lax.axis_size("member")
    slot_ids = jnp.arange(device_count, dtype=jnp.int32)
    dev_of_slot = (slot_ids % groups) * members + slot_ids // groups
    target_slot = (target_dev % members) * groups + target_dev // members
    picked = picked_dev[dev_of_slot]
    back_dest = back_dev[dev_of_slot]
    slot_pair = jnp.zeros((device_count,), jnp.int32).at[target_slot].set(
        jnp.arange(target_dev.shape[0], dtype=jnp.int32))
    slot_used = jnp.zeros((device_count,), jnp.int32).at[target_slot].set(1)
    h_order, h_starts = _lists(lhome, own_blocks)
    n_order, n_starts = _lists(lnear, own_blocks)
    r_order, r_starts = _lists(rhome, own_blocks)
    s_order, s_starts = _lists(back_dest, own_blocks)

    def apply_graph(blocks_in, init, extra=None, out_dtype=jnp.float32):
        send = build_send(picked, slot_pair, slot_used, rhome, blocks_in, remote_tiles, extra)
        recv = lax.all_to_all(send, SLOT_AXES, split_axis=0, concat_axis=0, tiled=True)
        part = local_sum(h_starts, h_order, n_starts, n_order, lhome, lnear, blocks_in, local_tiles, init)
        total = post_sum(r_starts, r_order, target_slot, s_starts, s_order, remote_tiles, recv, part,
                         out_dtype)
        return total.reshape(row_count, F), recv

    zeros = jnp.zeros((own_blocks, BLOCK, F), jnp.float32)
    aggregate = apply_graph(features.reshape(own_blocks, BLOCK, F), zeros, out_dtype=jnp.bfloat16)[0]
    joined = jnp.concatenate([features, aggregate], axis=1)
    pre_act = jnp.dot(joined, weight, preferred_element_type=jnp.float32)
    sigmoid_z = jax.nn.sigmoid(pre_act)
    output = (pre_act * sigmoid_z).astype(jnp.bfloat16)
    grad_pre = (
        cotangent.astype(jnp.float32) * sigmoid_z * (1.0 + pre_act * (1.0 - sigmoid_z))
    ).astype(jnp.bfloat16)
    partial_grad = jnp.einsum("ra,rf->af", joined, grad_pre, preferred_element_type=jnp.float32)
    rows = partial_grad.shape[0]
    chunk = rows // device_count
    pieces = partial_grad.reshape(device_count, chunk, F)[dev_of_slot]
    hi_f32 = lax.reduce_precision(pieces, exponent_bits=8, mantissa_bits=7)
    pieces_hi = hi_f32.astype(jnp.bfloat16)
    pieces_lo = (pieces - hi_f32).astype(jnp.bfloat16)
    extra = jnp.concatenate([pieces_hi, pieces_lo], axis=1)
    grad_self = jnp.einsum("rf,af->ra", grad_pre, weight[:F], preferred_element_type=jnp.float32)
    grad_nbr = jnp.einsum("rf,af->ra", grad_pre, weight[F:], preferred_element_type=jnp.float32)
    grad_agg = grad_nbr.astype(jnp.bfloat16).reshape(own_blocks, BLOCK, F)
    init_b = grad_self.reshape(own_blocks, BLOCK, F)
    grad_features, recv_b = apply_graph(grad_agg, init_b, extra)
    got = recv_b[:, 2 * BLOCK:, :].astype(jnp.float32)
    mine = jnp.sum(got[:, :chunk] + got[:, chunk:], axis=0)
    mine, grad_features = lax.optimization_barrier((mine, grad_features))
    grad_scale = 1.0 / math.sqrt(row_count * device_count)
    spread_out = jnp.broadcast_to(mine[None], (device_count, chunk, F))
    gathered = lax.all_to_all(spread_out, AXES, split_axis=0, concat_axis=0, tiled=True)
    grad_weight = gathered.reshape(rows, F) * grad_scale
    return (output, grad_weight, grad_features)


def solution(mesh):
    in_specs = (
        P(AXES, None),
        P(AXES),
        P(AXES),
        P(AXES, None, None),
        P(AXES),
        P(AXES),
        P(AXES, None, None),
        P(),
        P(AXES, None),
    )
    out_specs = (P(AXES, None), P(), P(AXES, None))
    return jax.shard_map(body, mesh=mesh, in_specs=in_specs, out_specs=out_specs, check_vma=False)
```

```python
import math

import jax
import jax.numpy as jnp
from jax import lax
from jax.experimental import pallas as pl
from jax.experimental.pallas import tpu as pltpu
from jax.sharding import PartitionSpec as P

F = 256
BLOCK = 128
BLK_DEV = 16
AXES = ("group", "member")
SLOT_AXES = ("member", "group")
VMEM_LIMIT = 56 * 1024 * 1024


def _smem():
    return pl.BlockSpec(memory_space=pltpu.SMEM)


def _vmem():
    return pl.BlockSpec(memory_space=pltpu.VMEM)


def _dot_t(a, v):
    return lax.dot_general(a, v, (((0,), (0,)), ((), ())), preferred_element_type=jnp.float32)


def _lists(dest, n_dest):
    order = jnp.argsort(dest, stable=True).astype(jnp.int32)
    counts = jnp.sum(dest[:, None] == jnp.arange(n_dest, dtype=jnp.int32)[None, :], axis=0)
    starts = jnp.concatenate([jnp.zeros((1,), jnp.int32), jnp.cumsum(counts).astype(jnp.int32)])
    return order, starts


def _pair_loop(lo, hi, term, acc):
    count = hi - lo
    iters = (count + 1) // 2

    def step(i, a):
        i0 = lo + 2 * i
        i1 = i0 + 1
        return a + term(i0, jnp.minimum(i1, hi - 1), i1 < hi)

    return lax.fori_loop(0, iters, step, acc)


def _local_kernel(hs_ref, ho_ref, ns_ref, no_ref, lh_ref, ln_ref, x_ref, lt_ref, init_ref, out_ref):
    blocks = out_ref.shape[0]

    def per_block(k, c):
        acc = init_ref[k]

        def home_term(i0, i1, ok):
            p0 = ho_ref[i0]
            p1 = ho_ref[i1]
            lhs = jnp.concatenate([lt_ref[p0], lt_ref[p1]], axis=1)
            v1 = jnp.where(ok, x_ref[ln_ref[p1]], jnp.zeros((BLOCK, F), x_ref.dtype))
            rhs = jnp.concatenate([x_ref[ln_ref[p0]], v1], axis=0)
            return jnp.dot(lhs, rhs, preferred_element_type=jnp.float32)

        acc = _pair_loop(hs_ref[k], hs_ref[k + 1], home_term, acc)

        def near_term(i0, i1, ok):
            p0 = no_ref[i0]
            p1 = no_ref[i1]
            lhs = jnp.concatenate([lt_ref[p0], lt_ref[p1]], axis=0)
            v1 = jnp.where(ok, x_ref[lh_ref[p1]], jnp.zeros((BLOCK, F), x_ref.dtype))
            rhs = jnp.concatenate([x_ref[lh_ref[p0]], v1], axis=0)
            return _dot_t(lhs, rhs)

        acc = _pair_loop(ns_ref[k], ns_ref[k + 1], near_term, acc)
        out_ref[k] = acc
        return c

    lax.fori_loop(0, blocks, per_block, 0)


def local_sum(hs, ho, ns, no, lh, ln, x, ltiles, init):
    pairs = ltiles.shape[0]
    cost = pl.CostEstimate(
        flops=2 * 2 * pairs * BLOCK * BLOCK * F,
        transcendentals=0,
        bytes_accessed=x.size * 2 + ltiles.size * 2 + init.size * 8,
    )
    return pl.pallas_call(
        _local_kernel,
        out_shape=jax.ShapeDtypeStruct(init.shape, jnp.float32),
        in_specs=[_smem()] * 6 + [_vmem()] * 3,
        out_specs=_vmem(),
        cost_estimate=cost,
        compiler_params=pltpu.CompilerParams(vmem_limit_bytes=VMEM_LIMIT),
    )(hs, ho, ns, no, lh, ln, x, ltiles, init)


SEND_GROUP = 64


def _send_kernel(picked_ref, spair_ref, sused_ref, rhome_ref, x_ref, rt_ref, *rest):
    send_ref = rest[-1]
    extra_ref = rest[0] if len(rest) == 2 else None
    group = send_ref.shape[0]
    base = pl.program_id(0) * group
    for j in range(group):
        t = base + j
        send_ref[j, pl.ds(0, BLOCK)] = x_ref[picked_ref[t]]
        p = spair_ref[t]
        r = _dot_t(rt_ref[p], x_ref[rhome_ref[p]])
        r = jnp.where(sused_ref[t] > 0, r, 0.0)
        send_ref[j, pl.ds(BLOCK, BLOCK)] = r.astype(send_ref.dtype)
        if extra_ref is not None:
            send_ref[j, pl.ds(2 * BLOCK, extra_ref.shape[1])] = extra_ref[j]


def build_send(picked, spair, sused, rhome, x, rtiles, extra=None):
    slots = picked.shape[0]
    group = math.gcd(SEND_GROUP, slots)
    full3 = lambda i: (0, 0, 0)
    extra_rows = 0 if extra is None else extra.shape[1]
    rows = 2 * BLOCK + extra_rows
    cost = pl.CostEstimate(
        flops=2 * slots * BLOCK * BLOCK * F,
        transcendentals=0,
        bytes_accessed=x.size * 2 + rtiles.size * 2 + slots * rows * F * 2,
    )
    in_specs = [_smem()] * 4 + [pl.BlockSpec(x.shape, full3), pl.BlockSpec(rtiles.shape, full3)]
    args = [picked, spair, sused, rhome, x, rtiles]
    if extra is not None:
        in_specs.append(pl.BlockSpec((group, extra_rows, F), lambda i: (i, 0, 0)))
        args.append(extra)
    return pl.pallas_call(
        _send_kernel,
        grid=(slots // group,),
        out_shape=jax.ShapeDtypeStruct((slots, rows, F), jnp.bfloat16),
        in_specs=in_specs,
        out_specs=pl.BlockSpec((group, rows, F), lambda i: (i, 0, 0)),
        cost_estimate=cost,
        compiler_params=pltpu.CompilerParams(vmem_limit_bytes=VMEM_LIMIT),
    )(*args)


def _post_kernel(rs_ref, ro_ref, td_ref, ss_ref, so_ref, rt_ref, recv_ref, base_ref, out_ref):
    blocks = out_ref.shape[0]

    def per_block(k, c):
        acc = base_ref[k]

        def remote_term(i0, i1, ok):
            p0 = ro_ref[i0]
            p1 = ro_ref[i1]
            lhs = jnp.concatenate([rt_ref[p0], rt_ref[p1]], axis=1)
            v1 = jnp.where(ok, recv_ref[td_ref[p1], pl.ds(0, BLOCK)], jnp.zeros((BLOCK, F), recv_ref.dtype))
            rhs = jnp.concatenate([recv_ref[td_ref[p0], pl.ds(0, BLOCK)], v1], axis=0)
            return jnp.dot(lhs, rhs, preferred_element_type=jnp.float32)

        acc = _pair_loop(rs_ref[k], rs_ref[k + 1], remote_term, acc)

        def back_term(i, a):
            return a + recv_ref[so_ref[i], pl.ds(BLOCK, BLOCK)].astype(jnp.float32)

        acc = lax.fori_loop(ss_ref[k], ss_ref[k + 1], back_term, acc)
        out_ref[k] = acc.astype(out_ref.dtype)
        return c

    lax.fori_loop(0, blocks, per_block, 0)


def post_sum(rs, ro, td, ss, so, rtiles, recv, base, out_dtype=jnp.float32):
    pairs = rtiles.shape[0]
    cost = pl.CostEstimate(
        flops=2 * pairs * BLOCK * BLOCK * F,
        transcendentals=0,
        bytes_accessed=rtiles.size * 2 + recv.size * 2 + base.size * 8,
    )
    return pl.pallas_call(
        _post_kernel,
        out_shape=jax.ShapeDtypeStruct(base.shape, out_dtype),
        in_specs=[_smem()] * 5 + [_vmem()] * 3,
        out_specs=_vmem(),
        cost_estimate=cost,
        input_output_aliases={7: 0} if out_dtype == base.dtype else {},
        compiler_params=pltpu.CompilerParams(vmem_limit_bytes=VMEM_LIMIT),
    )(rs, ro, td, ss, so, rtiles, recv, base)


def body(
    features,
    local_home,
    local_near,
    local_tiles,
    remote_home,
    remote_far,
    remote_tiles,
    weight,
    cotangent,
):
    device_count = lax.axis_size(AXES)
    row_count = features.shape[0]
    own_blocks = row_count // BLOCK
    lhome = jnp.clip(local_home, 0, own_blocks - 1)
    lnear = jnp.clip(local_near, 0, own_blocks - 1)
    rhome = jnp.clip(remote_home, 0, own_blocks - 1)
    target_dev = jnp.clip(remote_far // BLK_DEV, 0, device_count - 1)
    wanted = remote_far % BLK_DEV
    request = jnp.full((device_count,), -1, jnp.int32).at[target_dev].set(wanted)
    asked = lax.all_to_all(request, AXES, split_axis=0, concat_axis=0, tiled=True)
    picked_dev = jnp.clip(asked, 0, own_blocks - 1)
    back_dev = jnp.where(asked >= 0, picked_dev, own_blocks)
    groups = lax.axis_size("group")
    members = lax.axis_size("member")
    slot_ids = jnp.arange(device_count, dtype=jnp.int32)
    dev_of_slot = (slot_ids % groups) * members + slot_ids // groups
    target_slot = (target_dev % members) * groups + target_dev // members
    picked = picked_dev[dev_of_slot]
    back_dest = back_dev[dev_of_slot]
    slot_pair = jnp.zeros((device_count,), jnp.int32).at[target_slot].set(
        jnp.arange(target_dev.shape[0], dtype=jnp.int32))
    slot_used = jnp.zeros((device_count,), jnp.int32).at[target_slot].set(1)
    h_order, h_starts = _lists(lhome, own_blocks)
    n_order, n_starts = _lists(lnear, own_blocks)
    r_order, r_starts = _lists(rhome, own_blocks)
    s_order, s_starts = _lists(back_dest, own_blocks)

    def apply_graph(blocks_in, init, extra=None, out_dtype=jnp.float32):
        send = build_send(picked, slot_pair, slot_used, rhome, blocks_in, remote_tiles, extra)
        recv = lax.all_to_all(send, SLOT_AXES, split_axis=0, concat_axis=0, tiled=True)
        part = local_sum(h_starts, h_order, n_starts, n_order, lhome, lnear, blocks_in, local_tiles, init)
        total = post_sum(r_starts, r_order, target_slot, s_starts, s_order, remote_tiles, recv, part,
                         out_dtype)
        return total.reshape(row_count, F), recv

    zeros = jnp.zeros((own_blocks, BLOCK, F), jnp.float32)
    aggregate = apply_graph(features.reshape(own_blocks, BLOCK, F), zeros, out_dtype=jnp.bfloat16)[0]
    joined = jnp.concatenate([features, aggregate], axis=1)
    pre_act = jnp.dot(joined, weight, preferred_element_type=jnp.float32)
    sigmoid_z = jax.nn.sigmoid(pre_act)
    output = (pre_act * sigmoid_z).astype(jnp.bfloat16)
    grad_pre = (
        cotangent.astype(jnp.float32) * sigmoid_z * (1.0 + pre_act * (1.0 - sigmoid_z))
    ).astype(jnp.bfloat16)
    partial_grad = jnp.einsum("ra,rf->af", joined, grad_pre, preferred_element_type=jnp.float32)
    rows = partial_grad.shape[0]
    chunk = rows // device_count
    pieces = partial_grad.reshape(device_count, chunk, F)[dev_of_slot]
    hi_f32 = lax.reduce_precision(pieces, exponent_bits=8, mantissa_bits=7)
    pieces_hi = hi_f32.astype(jnp.bfloat16)
    pieces_lo = (pieces - hi_f32).astype(jnp.bfloat16)
    extra = jnp.concatenate([pieces_hi, pieces_lo], axis=1)
    grad_self = jnp.einsum("rf,af->ra", grad_pre, weight[:F], preferred_element_type=jnp.float32)
    grad_nbr = jnp.einsum("rf,af->ra", grad_pre, weight[F:], preferred_element_type=jnp.float32)
    grad_agg = grad_nbr.astype(jnp.bfloat16).reshape(own_blocks, BLOCK, F)
    init_b = grad_self.reshape(own_blocks, BLOCK, F)
    grad_features, recv_b = apply_graph(grad_agg, init_b, extra)
    got = recv_b[:, 2 * BLOCK:, :].astype(jnp.float32)
    mine = jnp.sum(got[:, :chunk] + got[:, chunk:], axis=0)
    mine, grad_features = lax.optimization_barrier((mine, grad_features))
    grad_scale = 1.0 / math.sqrt(row_count * device_count)
    spread_out = jnp.broadcast_to(mine[None], (device_count, chunk, F))
    gathered = lax.all_to_all(spread_out, AXES, split_axis=0, concat_axis=0, tiled=True)
    grad_weight = gathered.reshape(rows, F) * grad_scale
    return (output, grad_weight, grad_features)


def solution(mesh):
    in_specs = (
        P(AXES, None),
        P(AXES),
        P(AXES),
        P(AXES, None, None),
        P(AXES),
        P(AXES),
        P(AXES, None, None),
        P(),
        P(AXES, None),
    )
    out_specs = (P(AXES, None), P(), P(AXES, None))
    return jax.shard_map(body, mesh=mesh, in_specs=in_specs, out_specs=out_specs, check_vma=False)
```
